128 devices in a mesh: group: 4 (over x), expert: 32 (over y, z, core).
Axes of the slice: x: 4, y: 4, z: 4, core: 2. Of those that a mesh axis runs over, the one named last changes fastest.
Arguments:
- tokens: bfloat16 [16384, 2048], P(('group', 'expert')), may hold values from -6 to 6
- cotangent: bfloat16 [16384, 2048], P(('group', 'expert')), may hold values from -6 to 6
- gate_probs: float32 [16384, 8], P(('group', 'expert')), may hold values from 0.02 to 0.5
- expert_ids: int32 [16384, 8], P(('group', 'expert')), may hold values from 0 to 31, all different within a row; in each aligned block of 128 rows (0 to 127, 128 to 255, ...) at most 72 rows name the same one
- gate_up: bfloat16 [32, 2048, 768], P('expert'), may hold values from -0.125 to 0.125
- down_weight: bfloat16 [32, 384, 2048], P('expert'), may hold values from -0.3125 to 0.3125
- gate_up_moment: float32 [32, 2048, 768], P('expert', 'group'), may hold values from -6 to 6
- gate_up_second: float32 [32, 2048, 768], P('expert', 'group'), may hold values from 0.05 to 20
- down_moment: float32 [32, 384, 2048], P('expert', None, 'group'), may hold values from -6 to 6
- down_second: float32 [32, 384, 2048], P('expert', None, 'group'), may hold values from 0.05 to 20
Outputs:
- token_grad: bfloat16 [16384, 2048], P(('group', 'expert'))
- updated_gate_up: bfloat16 [32, 2048, 768], P('expert')
- updated_down: bfloat16 [32, 384, 2048], P('expert')
- gate_up_moment_out: float32 [32, 2048, 768], P('expert', 'group')
- gate_up_second_out: float32 [32, 2048, 768], P('expert', 'group')
- down_moment_out: float32 [32, 384, 2048], P('expert', None, 'group')
- down_second_out: float32 [32, 384, 2048], P('expert', None, 'group')
The draws below stay inside these ranges and needn't reach their ends.
Inputs may be any that keep to these rules, and one draw needn't show every extreme that they name: `expert_ids`: each row names 8 different experts. In the rows of one device no expert is named by more than 72 rows, and in every draw some expert is named by exactly 72 rows of some device.
All inputs are finite; a program needn't handle non-finite values.
Results may differ from the reference program's by a relative error of at most 0.015.
Values may be sent and summed in bfloat16 or wider, within the bound.
No kernel may reach another device: no remote copies, remote signals or barrier semaphores. Data moves between devices by JAX's collectives and lax.ppermute only.
A program may use at most 192 MiB of HBM per device.

```python
import math
import jax
import jax.numpy as jnp
import numpy as np
from jax import lax

D = 2048
HIDDEN_SIZE = 384
TOP = 8
TOK_DEV = 128
EXPERTS = 32
CAP = 72
TOKENS = 16384
N_GROUP = 4
N_EXPERT = 32


def levels(own_key, extent, pieces, low, largest):
    def one(position, blocks):
        draws = jax.random.uniform(jax.random.fold_in(jax.random.fold_in(own_key, 6), position), (blocks,), jnp.float32, low / len(pieces), largest / len(pieces))
        return jnp.repeat(jnp.exp(draws), extent[position] // blocks).reshape((-1,) + (1,) * (len(extent) - position - 1))

    level = one(*pieces[0])
    for cut in pieces[1:]:
        level = level * one(*cut)
    return level


def routed_block(key, own, number, rows, number_of, top, limit, lean):
    order = jax.random.permutation(key, number_of)
    crowded, common = load_shares(number_of, rows * top, limit, lean, True), load_shares(number_of, rows * top, limit, lean, False)
    places = jnp.arange(number_of)

    def named(sizes, offset_by):
        used = int((sizes > 0).sum())
        fixed = max(1, used // 4)
        passed = fixed + (places - fixed + offset_by * (used - fixed)) % max(1, number_of - fixed)
        return jnp.zeros((number_of,), jnp.int32).at[order[jnp.where(places < fixed, places, passed)]].set(jnp.asarray(sizes, jnp.int32))

    sizes = jnp.where(number % 4 == 0, named(crowded, number // 4), named(common, number - number // 4 - 1))
    mixed = jax.random.permutation(jax.random.fold_in(own, 3), number_of)
    donor, receiver = mixed[0:number_of // 2 * 2:2], mixed[1:number_of // 2 * 2:2]
    room = jnp.minimum(sizes[donor] - 1, limit - sizes[receiver]) // 2
    room = jnp.where((donor == order[0]) | (receiver == order[0]) | (sizes[receiver] == 0), 0, jnp.maximum(room, 0))
    passed = jax.random.randint(jax.random.fold_in(own, 4), (number_of // 2,), 0, 1 << 20) % (room + 1)
    sizes = sizes.at[donor].add(-passed).at[receiver].add(passed)
    members = jnp.searchsorted(jnp.cumsum(sizes), jnp.arange(rows * top), side="right").astype(jnp.int32)
    listing = members.reshape(top, rows).T
    listing = listing[jax.random.permutation(jax.random.fold_in(own, 1), rows)]
    offset_by = jax.random.randint(jax.random.fold_in(own, 2), (rows, 1), 0, top)
    return jnp.take_along_axis(listing, (jnp.arange(top)[None, :] + offset_by) % top, axis=1)


def load_shares(amount, total, reach, skew, full):
    weights = [(1 << 20) // math.isqrt(standing ** skew) + 1 for standing in range(1, amount + 1)]
    largest = reach if full else min(reach, max(-(-total // amount), total * weights[0] // sum(weights)))
    least = 1 if total - largest >= amount - 1 else 0
    holding, surplus = [largest] + [least] * (amount - 1), total - largest - least * (amount - 1)
    while surplus > 0:
        free = [i for i in range(1, amount) if holding[i] < largest] or [i for i in range(1, amount) if holding[i] < reach]
        pool, left = sum([weights[i] for i in free]), surplus
        for i in free:
            more = min(reach - holding[i], max(1, left * weights[i] // pool), surplus)
            holding[i] = holding[i] + more
            surplus = surplus - more
    return np.array(holding)


def scatter_about(own_key, extent, width, limit, pieces=(), kind=jnp.bfloat16):
    result = jax.random.normal(own_key, extent, jnp.float32) * width
    if len(pieces) > 0:
        result = levels(own_key, extent, pieces, -0.22, 0.18) * result
    return jnp.clip(result, min=-limit, max=limit).astype(kind)


def setup_inputs(seed: int = 0) -> dict:
    splits = jax.random.split(jax.random.key(seed), 11)
    tokens = scatter_about(splits[0], (TOKENS, D), 1.0, 6.0, ((0, 128),))
    cotangent = scatter_about(splits[1], (TOKENS, D), 1.0, 6.0, ((0, 128),))
    gate_probs = jnp.clip(jnp.exp(math.log(0.5) - 3.218876 * jax.random.uniform(splits[2], (TOKENS, TOP), jnp.float32) ** levels(splits[2], (TOKENS, TOP), ((0, 128),), -0.2, 0.2)), 0.02, 0.5)
    expert_ids_keys = jax.random.split(jax.random.fold_in(splits[3], 1), TOKENS // TOK_DEV)
    expert_ids_turns = jax.random.permutation(jax.random.fold_in(splits[3], 3), TOKENS // TOK_DEV)
    expert_ids = jax.vmap(lambda own, number: routed_block(jax.random.fold_in(splits[3], 2), own, number, TOK_DEV, EXPERTS, TOP, CAP, 1))(expert_ids_keys, expert_ids_turns).reshape((TOKENS, TOP))
    gate_up = scatter_about(splits[4], (EXPERTS, D, 2 * HIDDEN_SIZE), D ** -0.5, 0.125, ((0, 32),))
    down_weight = scatter_about(splits[5], (EXPERTS, HIDDEN_SIZE, D), HIDDEN_SIZE ** -0.5, 0.3125, ((0, 32),))
    gate_up_moment = scatter_about(splits[6], (EXPERTS, D, 2 * HIDDEN_SIZE), 1.0, 6.0, ((0, 32), (1, 4)), jnp.float32)
    gate_up_second = jnp.clip(jnp.exp(math.log(20.0) - 5.9914645 * jax.random.uniform(splits[7], (EXPERTS, D, 2 * HIDDEN_SIZE), jnp.float32) ** levels(splits[7], (EXPERTS, D, 2 * HIDDEN_SIZE), ((0, 32), (1, 4)), -0.2, 0.2)), 0.05, 20.0)
    down_moment = scatter_about(splits[8], (EXPERTS, HIDDEN_SIZE, D), 1.0, 6.0, ((0, 32), (2, 4)), jnp.float32)
    down_second = jnp.clip(jnp.exp(math.log(20.0) - 5.9914645 * jax.random.uniform(splits[9], (EXPERTS, HIDDEN_SIZE, D), jnp.float32) ** levels(splits[9], (EXPERTS, HIDDEN_SIZE, D), ((0, 32), (2, 4)), -0.2, 0.2)), 0.05, 20.0)
    return dict(tokens=tokens, cotangent=cotangent, gate_probs=gate_probs, expert_ids=expert_ids, gate_up=gate_up, down_weight=down_weight, gate_up_moment=gate_up_moment, gate_up_second=gate_up_second, down_moment=down_moment, down_second=down_second)


learn_rate = 0.001
beta_first = 0.9
beta_second = 0.999
adam_eps = 1e-08

def expert_backward(inputs, scaled_grad, weight_gate_up, weight_down):
    hidden_count = weight_down.shape[0]
    projected = jnp.dot(inputs, weight_gate_up, preferred_element_type=jnp.float32)
    gate_part = projected[:, :hidden_count]
    up_part = projected[:, hidden_count:]
    sigmoid_gate = jax.nn.sigmoid(gate_part)
    activated = gate_part * sigmoid_gate
    hidden_act = (activated * up_part).astype(jnp.bfloat16)
    hidden_grad = jnp.dot(scaled_grad, weight_down.T, preferred_element_type=jnp.float32)
    slope = sigmoid_gate * (1.0 + gate_part * (1.0 - sigmoid_gate))
    pair_grad = jnp.concatenate([hidden_grad * up_part * slope, hidden_grad * activated], axis=1).astype(jnp.bfloat16)
    down_grad = jnp.dot(hidden_act.T, scaled_grad, preferred_element_type=jnp.float32)
    gate_up_grad = jnp.dot(inputs.T, pair_grad, preferred_element_type=jnp.float32)
    input_grad = jnp.dot(pair_grad, weight_gate_up.T, preferred_element_type=jnp.float32).astype(jnp.bfloat16)
    return (gate_up_grad, down_grad, input_grad)

def adam_update(weight, grad, first, second):
    first_new = beta_first * first + (1.0 - beta_first) * grad
    second_new = beta_second * second + (1.0 - beta_second) * grad * grad
    updated = (weight.astype(jnp.float32) - learn_rate * first_new / (jnp.sqrt(second_new) + adam_eps)).astype(jnp.bfloat16)
    return (updated, first_new, second_new)

def reference(tokens, cotangent, gate_probs, expert_ids, gate_up, down_weight, gate_up_moment, gate_up_second, down_moment, down_second):
    devices = N_GROUP * N_EXPERT
    per_device = TOK_DEV * TOP
    flat_ids = expert_ids.reshape(devices, per_device)
    onehot = (flat_ids[:, :, None] == jnp.arange(EXPERTS, dtype=jnp.int32)[None, None, :]).astype(jnp.int32)
    before = jnp.cumsum(onehot, axis=1) - onehot
    slot_rank = lax.optimization_barrier(jnp.sum(before * onehot, axis=2)).astype(jnp.int32)
    slot_index = (flat_ids * CAP + slot_rank).astype(jnp.int32)
    source_rows = jnp.broadcast_to(jnp.arange(devices, dtype=jnp.int32)[:, None], (devices, per_device))
    pair_ids = jnp.broadcast_to(jnp.arange(per_device, dtype=jnp.int32)[None, :], (devices, per_device))
    table = jnp.full((devices, EXPERTS * CAP), -1, jnp.int32).at[source_rows, slot_index].set(pair_ids)
    table = table.reshape(devices, EXPERTS, CAP)
    owners = jnp.repeat(jnp.arange(devices, dtype=jnp.int32), CAP)

    def per_expert(accum, expert_index):
        entries = lax.dynamic_index_in_dim(table, expert_index, 1, keepdims=False).reshape(-1)
        usable = entries >= 0
        clamped = jnp.where(usable, entries, 0).astype(jnp.int32)
        token_index = (owners * TOK_DEV + clamped // TOP).astype(jnp.int32)
        pick_index = (clamped % TOP).astype(jnp.int32)
        inputs = jnp.where(usable[:, None], tokens[token_index], jnp.zeros((), jnp.bfloat16))
        weights = jnp.where(usable, gate_probs[token_index, pick_index], jnp.zeros((), jnp.float32))
        scaled = (weights[:, None] * cotangent[token_index].astype(jnp.float32)).astype(jnp.bfloat16)
        grad_pair, grad_down, input_grad = expert_backward(inputs, scaled, gate_up[expert_index], down_weight[expert_index])
        accum = accum.at[token_index].add(jnp.where(usable[:, None], input_grad.astype(jnp.float32), jnp.zeros((), jnp.float32)))
        return (accum, (grad_pair, grad_down))
    start = jnp.zeros((TOKENS, D), jnp.float32)
    accum, grads = lax.scan(per_expert, start, jnp.arange(EXPERTS, dtype=jnp.int32))
    grad_pair, grad_down = grads
    new_gate_up, first_gate_up, second_gate_up = adam_update(gate_up, grad_pair, gate_up_moment, gate_up_second)
    new_down, first_down, second_down = adam_update(down_weight, grad_down, down_moment, down_second)
    return (accum.astype(jnp.bfloat16), new_gate_up, new_down, first_gate_up, second_gate_up, first_down, second_down)
```

```python
import jax
import jax.numpy as jnp
from jax import lax
from jax.sharding import PartitionSpec as P

learn_rate = 0.001
beta_first = 0.9
beta_second = 0.999
adam_eps = 1e-08


def expert_backward(inputs, scaled_grad, weight_gate_up, weight_down):
    hidden_count = weight_down.shape[0]
    projected = jnp.dot(inputs, weight_gate_up, preferred_element_type=jnp.float32)
    gate_part = projected[:, :hidden_count]
    up_part = projected[:, hidden_count:]
    sigmoid_gate = jax.nn.sigmoid(gate_part)
    activated = gate_part * sigmoid_gate
    hidden_act = (activated * up_part).astype(jnp.bfloat16)
    hidden_grad = jnp.dot(scaled_grad, weight_down.T, preferred_element_type=jnp.float32)
    slope = sigmoid_gate * (1.0 + gate_part * (1.0 - sigmoid_gate))
    pair_grad = jnp.concatenate(
        [hidden_grad * up_part * slope, hidden_grad * activated], axis=1
    ).astype(jnp.bfloat16)
    down_grad = jnp.dot(hidden_act.T, scaled_grad, preferred_element_type=jnp.float32)
    gate_up_grad = jnp.dot(inputs.T, pair_grad, preferred_element_type=jnp.float32)
    input_grad = jnp.dot(pair_grad, weight_gate_up.T, preferred_element_type=jnp.float32).astype(
        jnp.bfloat16
    )
    return (gate_up_grad, down_grad, input_grad)


def adam_update(weight, grad, first, second):
    first_new = beta_first * first + (1.0 - beta_first) * grad
    second_new = beta_second * second + (1.0 - beta_second) * grad * grad
    updated = (
        weight.astype(jnp.float32) - learn_rate * first_new / (jnp.sqrt(second_new) + adam_eps)
    ).astype(jnp.bfloat16)
    return (updated, first_new, second_new)


def exclusive_count(flags):
    n = flags.shape[-1]
    earlier = (jnp.arange(n)[:, None] < jnp.arange(n)[None, :]).astype(jnp.bfloat16)
    return jnp.dot(flags.astype(jnp.bfloat16), earlier, preferred_element_type=jnp.float32)


def local(
    tokens,
    cotangent,
    gate_probs,
    expert_ids,
    gate_up,
    down_weight,
    gate_up_moment,
    gate_up_second,
    down_moment,
    down_second,
):
    expert_count = lax.axis_size("expert")
    me = lax.axis_index("expert")
    local_tokens, model_width = tokens.shape
    top_count = expert_ids.shape[1]
    capacity = min(local_tokens, 9 * local_tokens * top_count // (4 * expert_count))
    slot_total = expert_count * capacity

    all_tokens = lax.all_gather(tokens, "expert", axis=0)
    all_cot = lax.all_gather(cotangent, "expert", axis=0)
    meta = jnp.concatenate([expert_ids.astype(jnp.float32), gate_probs], axis=1)
    all_meta = lax.all_gather(meta, "expert", axis=0)
    all_ids = all_meta[..., :top_count].astype(jnp.int32)
    all_gates = all_meta[..., top_count:]

    match = all_ids == me
    routed = jnp.any(match, axis=-1).astype(jnp.float32)
    gate_of = jnp.sum(jnp.where(match, all_gates, 0.0), axis=-1)
    rank = exclusive_count(routed)
    slots = jnp.arange(capacity, dtype=jnp.float32)
    pick = (routed[:, None, :] > 0) & (rank[:, None, :] == slots[None, :, None])
    pick_b = pick.astype(jnp.bfloat16)
    inputs = jnp.einsum(
        "srt,stc->src", pick_b, all_tokens, preferred_element_type=jnp.float32
    ).astype(jnp.bfloat16)
    cot_rows = jnp.einsum(
        "srt,stc->src", pick_b, all_cot, preferred_element_type=jnp.float32
    )
    slot_gate = jnp.sum(jnp.where(pick, gate_of[:, None, :], 0.0), axis=-1)
    scaled = (slot_gate[..., None] * cot_rows).astype(jnp.bfloat16)

    weight_pair = gate_up[0]
    weight_down = down_weight[0]
    grad_pair, grad_down, row_grads = expert_backward(
        inputs.reshape(slot_total, model_width),
        scaled.reshape(slot_total, model_width),
        weight_pair,
        weight_down,
    )
    returned = lax.all_to_all(
        row_grads.reshape(expert_count, capacity, model_width),
        "expert",
        split_axis=0,
        concat_axis=0,
        tiled=True,
    )

    own_match = (
        expert_ids[:, :, None] == jnp.arange(expert_count, dtype=jnp.int32)[None, None, :]
    )
    own_routed = jnp.any(own_match, axis=1).astype(jnp.float32)
    own_rank = exclusive_count(own_routed.T).T
    own_pick = (own_routed[:, :, None] > 0) & (
        own_rank[:, :, None] == slots[None, None, :]
    )
    own_pick = own_pick.astype(jnp.bfloat16).reshape(local_tokens, slot_total)
    token_grad = jnp.dot(
        own_pick, returned.reshape(slot_total, model_width), preferred_element_type=jnp.float32
    ).astype(jnp.bfloat16)

    sum_pair, sum_down = (
        lax.psum_scatter(
            grad_pair[None].astype(jnp.bfloat16), "group", scatter_dimension=1, tiled=True
        ).astype(jnp.float32),
        lax.psum_scatter(
            grad_down[None].astype(jnp.bfloat16), "group", scatter_dimension=2, tiled=True
        ).astype(jnp.float32),
    )
    group_index = lax.axis_index("group")
    share_rows = model_width // lax.axis_size("group")
    own_pair = lax.dynamic_slice_in_dim(gate_up, group_index * share_rows, share_rows, 1)
    own_down = lax.dynamic_slice_in_dim(down_weight, group_index * share_rows, share_rows, 2)
    new_pair, first_pair, second_pair = adam_update(
        own_pair, sum_pair, gate_up_moment, gate_up_second
    )
    new_down, first_down, second_down = adam_update(own_down, sum_down, down_moment, down_second)
    full_pair, full_down = (
        lax.all_gather(new_pair, "group", axis=1, tiled=True),
        lax.all_gather(new_down, "group", axis=2, tiled=True),
    )
    return (token_grad, full_pair, full_down, first_pair, second_pair, first_down, second_down)


def solution(mesh):
    rows = P(("group", "expert"), None)
    placed = (
        rows,
        rows,
        rows,
        rows,
        P("expert", None, None),
        P("expert", None, None),
        P("expert", "group", None),
        P("expert", "group", None),
        P("expert", None, "group"),
        P("expert", None, "group"),
    )
    return jax.shard_map(
        local,
        mesh=mesh,
        in_specs=placed,
        out_specs=(
            rows,
            P("expert", None, None),
            P("expert", None, None),
            P("expert", "group", None),
            P("expert", "group", None),
            P("expert", None, "group"),
            P("expert", None, "group"),
        ),
        check_vma=False,
    )
```

```python
import jax
import jax.numpy as jnp
from jax import lax
from jax.sharding import Mesh, PartitionSpec as P

learn_rate = 0.001
beta_first = 0.9
beta_second = 0.999
adam_eps = 1e-08


def expert_backward(inputs, scaled_grad, weight_gate_up, weight_down):
    hidden_count = weight_down.shape[0]
    projected = jnp.dot(inputs, weight_gate_up, preferred_element_type=jnp.float32)
    gate_part = projected[:, :hidden_count]
    up_part = projected[:, hidden_count:]
    sigmoid_gate = jax.nn.sigmoid(gate_part)
    activated = gate_part * sigmoid_gate
    hidden_act = (activated * up_part).astype(jnp.bfloat16)
    hidden_grad = jnp.dot(scaled_grad, weight_down.T, preferred_element_type=jnp.float32)
    slope = sigmoid_gate * (1.0 + gate_part * (1.0 - sigmoid_gate))
    pair_grad = jnp.concatenate(
        [hidden_grad * up_part * slope, hidden_grad * activated], axis=1
    ).astype(jnp.bfloat16)
    down_grad = jnp.dot(hidden_act.T, scaled_grad, preferred_element_type=jnp.float32)
    gate_up_grad = jnp.dot(inputs.T, pair_grad, preferred_element_type=jnp.float32)
    input_grad = jnp.dot(pair_grad, weight_gate_up.T, preferred_element_type=jnp.float32).astype(
        jnp.bfloat16
    )
    return (gate_up_grad, down_grad, input_grad)


def adam_update(weight, grad, first, second):
    first_new = beta_first * first + (1.0 - beta_first) * grad
    second_new = beta_second * second + (1.0 - beta_second) * grad * grad
    updated = (
        weight.astype(jnp.float32) - learn_rate * first_new / (jnp.sqrt(second_new) + adam_eps)
    ).astype(jnp.bfloat16)
    return (updated, first_new, second_new)


def exclusive_count(flags):
    n = flags.shape[-1]
    earlier = (jnp.arange(n)[:, None] < jnp.arange(n)[None, :]).astype(jnp.bfloat16)
    return jnp.dot(flags.astype(jnp.bfloat16), earlier, preferred_element_type=jnp.float32)


def local(
    tokens,
    cotangent,
    gate_probs,
    expert_ids,
    gate_up,
    down_weight,
    gate_up_moment,
    gate_up_second,
    down_moment,
    down_second,
):
    chips = lax.axis_size("chip")
    cores = lax.axis_size("core")
    my_chip = lax.axis_index("chip")
    my_core = lax.axis_index("core")
    me = my_chip * cores + my_core
    expert_count = chips * cores
    local_tokens, model_width = tokens.shape
    top_count = expert_ids.shape[1]
    capacity = min(local_tokens, 9 * local_tokens * top_count // (4 * expert_count))
    half_slots = chips * capacity
    swap = [(0, 1), (1, 0)]
    slots = jnp.arange(capacity, dtype=jnp.float32)

    tok_near = lax.all_gather(tokens, "chip", axis=0)
    cot_near = lax.all_gather(cotangent, "chip", axis=0)
    meta = jnp.concatenate([expert_ids.astype(jnp.float32), gate_probs], axis=1)
    meta_near = lax.all_gather(meta, "chip", axis=0)
    meta_far = lax.ppermute(meta_near, "core", swap)
    tok_far = lax.ppermute(tok_near, "core", swap)
    cot_far = lax.ppermute(cot_near, "core", swap)

    def pick_rows(meta_blk, tok_blk, cot_blk):
        ids = meta_blk[..., :top_count].astype(jnp.int32)
        gates = meta_blk[..., top_count:]
        match = ids == me
        routed = jnp.any(match, axis=-1).astype(jnp.float32)
        gate_of = jnp.sum(jnp.where(match, gates, 0.0), axis=-1)
        rank = exclusive_count(routed)
        pick = (routed[:, None, :] > 0) & (rank[:, None, :] == slots[None, :, None])
        pick_b = pick.astype(jnp.bfloat16)
        inputs = jnp.einsum(
            "srt,stc->src", pick_b, tok_blk, preferred_element_type=jnp.float32
        ).astype(jnp.bfloat16)
        cot_rows = jnp.einsum("srt,stc->src", pick_b, cot_blk, preferred_element_type=jnp.float32)
        slot_gate = jnp.sum(jnp.where(pick, gate_of[:, None, :], 0.0), axis=-1)
        scaled = (slot_gate[..., None] * cot_rows).astype(jnp.bfloat16)
        return inputs.reshape(half_slots, model_width), scaled.reshape(half_slots, model_width)

    weight_pair = gate_up[0]
    weight_down = down_weight[0]
    rows_near, scaled_near = pick_rows(meta_near, tok_near, cot_near)
    pair_near, down_near, grads_near = expert_backward(rows_near, scaled_near, weight_pair, weight_down)
    back_near = lax.all_to_all(
        grads_near.reshape(chips, capacity, model_width), "chip", 0, 0, tiled=True
    )
    rows_far, scaled_far = pick_rows(meta_far, tok_far, cot_far)
    pair_far, down_far, grads_far = expert_backward(rows_far, scaled_far, weight_pair, weight_down)
    handed = lax.ppermute(grads_far.reshape(chips, capacity, model_width), "core", swap)
    back_far = lax.all_to_all(handed, "chip", 0, 0, tiled=True)
    grad_pair = pair_near + pair_far
    grad_down = down_near + down_far

    chip_ids = jnp.arange(chips, dtype=jnp.int32) * cores

    def combine(expert_of, back):
        match = jnp.any(expert_ids[:, :, None] == expert_of[None, None, :], axis=1)
        routed = match.astype(jnp.float32)
        rank = exclusive_count(routed.T).T
        pick = match[:, :, None] & (rank[:, :, None] == slots[None, None, :])
        pick = pick.astype(jnp.bfloat16).reshape(local_tokens, half_slots)
        return jnp.dot(
            pick, back.reshape(half_slots, model_width), preferred_element_type=jnp.float32
        )

    token_grad = (
        combine(chip_ids + my_core, back_near) + combine(chip_ids + (1 - my_core), back_far)
    ).astype(jnp.bfloat16)

    sum_pair, sum_down = (
        lax.psum_scatter(
            grad_pair[None].astype(jnp.bfloat16), "group", scatter_dimension=1, tiled=True
        ).astype(jnp.float32),
        lax.psum_scatter(
            grad_down[None].astype(jnp.bfloat16), "group", scatter_dimension=2, tiled=True
        ).astype(jnp.float32),
    )
    group_index = lax.axis_index("group")
    share_rows = model_width // lax.axis_size("group")
    own_pair = lax.dynamic_slice_in_dim(gate_up, group_index * share_rows, share_rows, 1)
    own_down = lax.dynamic_slice_in_dim(down_weight, group_index * share_rows, share_rows, 2)
    new_pair, first_pair, second_pair = adam_update(
        own_pair, sum_pair, gate_up_moment, gate_up_second
    )
    new_down, first_down, second_down = adam_update(own_down, sum_down, down_moment, down_second)
    full_pair, full_down = (
        lax.all_gather(new_pair, "group", axis=1, tiled=True),
        lax.all_gather(new_down, "group", axis=2, tiled=True),
    )
    return (token_grad, full_pair, full_down, first_pair, second_pair, first_down, second_down)


def solution(mesh):
    groups, experts = mesh.devices.shape
    split = Mesh(mesh.devices.reshape(groups, experts // 2, 2), ("group", "chip", "core"))
    rows = P(("group", "chip", "core"), None)
    expert_dim = ("chip", "core")
    placed = (
        rows,
        rows,
        rows,
        rows,
        P(expert_dim, None, None),
        P(expert_dim, None, None),
        P(expert_dim, "group", None),
        P(expert_dim, "group", None),
        P(expert_dim, None, "group"),
        P(expert_dim, None, "group"),
    )
    return jax.shard_map(
        local,
        mesh=split,
        in_specs=placed,
        out_specs=(
            rows,
            P(expert_dim, None, None),
            P(expert_dim, None, None),
            P(expert_dim, "group", None),
            P(expert_dim, "group", None),
            P(expert_dim, None, "group"),
            P(expert_dim, None, "group"),
        ),
        check_vma=False,
    )
```

```python
import jax
import jax.numpy as jnp
from jax import lax
from jax.sharding import PartitionSpec as P

learn_rate = 0.001
beta_first = 0.9
beta_second = 0.999
adam_eps = 1e-08


def expert_backward(inputs, scaled_grad, weight_gate_up, weight_down):
    hidden_count = weight_down.shape[0]
    projected = jnp.dot(inputs, weight_gate_up, preferred_element_type=jnp.float32)
    gate_part = projected[:, :hidden_count]
    up_part = projected[:, hidden_count:]
    sigmoid_gate = jax.nn.sigmoid(gate_part)
    activated = gate_part * sigmoid_gate
    hidden_act = (activated * up_part).astype(jnp.bfloat16)
    hidden_grad = jnp.dot(scaled_grad, weight_down.T, preferred_element_type=jnp.float32)
    slope = sigmoid_gate * (1.0 + gate_part * (1.0 - sigmoid_gate))
    pair_grad = jnp.concatenate(
        [hidden_grad * up_part * slope, hidden_grad * activated], axis=1
    ).astype(jnp.bfloat16)
    down_grad = jnp.dot(hidden_act.T, scaled_grad, preferred_element_type=jnp.float32)
    gate_up_grad = jnp.dot(inputs.T, pair_grad, preferred_element_type=jnp.float32)
    input_grad = jnp.dot(pair_grad, weight_gate_up.T, preferred_element_type=jnp.float32).astype(
        jnp.bfloat16
    )
    return (gate_up_grad, down_grad, input_grad)


def adam_update(weight, grad, first, second):
    first_new = beta_first * first + (1.0 - beta_first) * grad
    second_new = beta_second * second + (1.0 - beta_second) * grad * grad
    updated = (
        weight.astype(jnp.float32) - learn_rate * first_new / (jnp.sqrt(second_new) + adam_eps)
    ).astype(jnp.bfloat16)
    return (updated, first_new, second_new)


def exclusive_count(flags):
    n = flags.shape[-1]
    earlier = (jnp.arange(n)[:, None] < jnp.arange(n)[None, :]).astype(jnp.bfloat16)
    return jnp.dot(flags.astype(jnp.bfloat16), earlier, preferred_element_type=jnp.float32)


def local(
    tokens,
    cotangent,
    gate_probs,
    expert_ids,
    gate_up,
    down_weight,
    gate_up_moment,
    gate_up_second,
    down_moment,
    down_second,
):
    expert_count = lax.axis_size("expert")
    me = lax.axis_index("expert")
    local_tokens, model_width = tokens.shape
    top_count = expert_ids.shape[1]
    capacity = min(local_tokens, 9 * local_tokens * top_count // (4 * expert_count))
    slot_total = expert_count * capacity

    all_tokens = lax.all_gather(tokens, "expert", axis=0)
    all_cot = lax.all_gather(cotangent, "expert", axis=0)
    meta = jnp.concatenate([expert_ids.astype(jnp.float32), gate_probs], axis=1)
    all_meta = lax.all_gather(meta, "expert", axis=0)
    all_ids = all_meta[..., :top_count].astype(jnp.int32)
    all_gates = all_meta[..., top_count:]

    match = all_ids == me
    routed = jnp.any(match, axis=-1).astype(jnp.float32)
    gate_of = jnp.sum(jnp.where(match, all_gates, 0.0), axis=-1)
    rank = exclusive_count(routed)
    slots = jnp.arange(capacity, dtype=jnp.float32)
    pick = (routed[:, None, :] > 0) & (rank[:, None, :] == slots[None, :, None])
    pick_b = pick.astype(jnp.bfloat16)
    inputs = jnp.einsum(
        "srt,stc->src", pick_b, all_tokens, preferred_element_type=jnp.float32
    ).astype(jnp.bfloat16)
    cot_rows = jnp.einsum(
        "srt,stc->src", pick_b, all_cot, preferred_element_type=jnp.float32
    )
    slot_gate = jnp.sum(jnp.where(pick, gate_of[:, None, :], 0.0), axis=-1)
    scaled = (slot_gate[..., None] * cot_rows).astype(jnp.bfloat16)

    weight_pair = gate_up[0]
    weight_down = down_weight[0]
    grad_pair, grad_down, row_grads = expert_backward(
        inputs.reshape(slot_total, model_width),
        scaled.reshape(slot_total, model_width),
        weight_pair,
        weight_down,
    )
    dense = jnp.einsum(
        "srt,src->stc",
        pick_b,
        row_grads.reshape(expert_count, capacity, model_width),
        preferred_element_type=jnp.float32,
    ).astype(jnp.bfloat16)
    token_grad = lax.psum_scatter(
        dense.reshape(expert_count * local_tokens, model_width),
        "expert",
        scatter_dimension=0,
        tiled=True,
    )

    groups = lax.axis_size("group")
    share_rows = model_width // groups
    hidden_count = grad_down.shape[0]
    pair_size = share_rows * grad_pair.shape[1]
    down_size = hidden_count * share_rows
    pair_parts = grad_pair.astype(jnp.bfloat16).reshape(groups, pair_size)
    down_parts = (
        grad_down.astype(jnp.bfloat16)
        .reshape(hidden_count, groups, share_rows)
        .transpose(1, 0, 2)
        .reshape(groups, down_size)
    )
    parts = lax.all_to_all(
        jnp.concatenate([pair_parts, down_parts], axis=1), "group", 0, 0, tiled=True
    )
    summed = jnp.sum(parts.astype(jnp.float32), axis=0)
    sum_pair = summed[:pair_size].reshape(1, share_rows, grad_pair.shape[1])
    sum_down = summed[pair_size:].reshape(1, hidden_count, share_rows)
    group_index = lax.axis_index("group")
    own_pair = lax.dynamic_slice_in_dim(gate_up, group_index * share_rows, share_rows, 1)
    own_down = lax.dynamic_slice_in_dim(down_weight, group_index * share_rows, share_rows, 2)
    new_pair, first_pair, second_pair = adam_update(
        own_pair, sum_pair, gate_up_moment, gate_up_second
    )
    new_down, first_down, second_down = adam_update(own_down, sum_down, down_moment, down_second)
    packed = jnp.concatenate([new_pair.reshape(1, pair_size), new_down.reshape(1, down_size)], axis=1)
    shared = lax.all_to_all(
        jnp.broadcast_to(packed, (groups, pair_size + down_size)), "group", 0, 0, tiled=True
    )
    full_pair = shared[:, :pair_size].reshape(1, model_width, grad_pair.shape[1])
    full_down = (
        shared[:, pair_size:]
        .reshape(groups, hidden_count, share_rows)
        .transpose(1, 0, 2)
        .reshape(1, hidden_count, model_width)
    )
    return (token_grad, full_pair, full_down, first_pair, second_pair, first_down, second_down)


def solution(mesh):
    rows = P(("group", "expert"), None)
    placed = (
        rows,
        rows,
        rows,
        rows,
        P("expert", None, None),
        P("expert", None, None),
        P("expert", "group", None),
        P("expert", "group", None),
        P("expert", None, "group"),
        P("expert", None, "group"),
    )
    return jax.shard_map(
        local,
        mesh=mesh,
        in_specs=placed,
        out_specs=(
            rows,
            P("expert", None, None),
            P("expert", None, None),
            P("expert", "group", None),
            P("expert", "group", None),
            P("expert", None, "group"),
            P("expert", None, "group"),
        ),
        check_vma=False,
    )
```

```python
import jax
import jax.numpy as jnp
from jax import lax
from jax.sharding import PartitionSpec as P

learn_rate = 0.001
beta_first = 0.9
beta_second = 0.999
adam_eps = 1e-08


def expert_backward(inputs, scaled_grad, weight_gate_up, weight_down):
    hidden_count = weight_down.shape[0]
    projected = jnp.dot(inputs, weight_gate_up, preferred_element_type=jnp.float32)
    gate_part = projected[:, :hidden_count]
    up_part = projected[:, hidden_count:]
    sigmoid_gate = jax.nn.sigmoid(gate_part)
    activated = gate_part * sigmoid_gate
    hidden_act = (activated * up_part).astype(jnp.bfloat16)
    hidden_grad = jnp.dot(scaled_grad, weight_down.T, preferred_element_type=jnp.float32)
    slope = sigmoid_gate * (1.0 + gate_part * (1.0 - sigmoid_gate))
    hidden_act, up_slope, activated = lax.optimization_barrier(
        (hidden_act, up_part * slope, activated)
    )
    pair_grad = jnp.concatenate(
        [hidden_grad * up_slope, hidden_grad * activated], axis=1
    ).astype(jnp.bfloat16)
    down_grad = jnp.dot(hidden_act.T, scaled_grad, preferred_element_type=jnp.float32)
    gate_up_grad = jnp.dot(inputs.T, pair_grad, preferred_element_type=jnp.float32)
    input_grad = jnp.dot(pair_grad, weight_gate_up.T, preferred_element_type=jnp.float32).astype(
        jnp.bfloat16
    )
    return (gate_up_grad, down_grad, input_grad)


def adam_update(weight, grad, first, second):
    first_new = beta_first * first + (1.0 - beta_first) * grad
    second_new = beta_second * second + (1.0 - beta_second) * grad * grad
    updated = (
        weight.astype(jnp.float32) - learn_rate * first_new / (jnp.sqrt(second_new) + adam_eps)
    ).astype(jnp.bfloat16)
    return (updated, first_new, second_new)


def exclusive_count(flags):
    n = flags.shape[-1]
    earlier = (jnp.arange(n)[:, None] < jnp.arange(n)[None, :]).astype(jnp.bfloat16)
    return jnp.dot(flags.astype(jnp.bfloat16), earlier, preferred_element_type=jnp.float32)


def local(
    tokens,
    cotangent,
    gate_probs,
    expert_ids,
    gate_up,
    down_weight,
    gate_up_moment,
    gate_up_second,
    down_moment,
    down_second,
):
    expert_count = lax.axis_size("expert")
    me = lax.axis_index("expert")
    local_tokens, model_width = tokens.shape
    top_count = expert_ids.shape[1]
    capacity = min(local_tokens, 9 * local_tokens * top_count // (4 * expert_count))
    slot_total = expert_count * capacity

    all_tokens = lax.all_gather(tokens, "expert", axis=0)
    all_cot = lax.all_gather(cotangent, "expert", axis=0)
    meta = jnp.concatenate([expert_ids.astype(jnp.float32), gate_probs], axis=1)
    all_meta = lax.all_gather(meta, "expert", axis=0)
    all_ids = all_meta[..., :top_count].astype(jnp.int32)
    all_gates = all_meta[..., top_count:]

    match = all_ids == me
    routed = jnp.any(match, axis=-1).astype(jnp.float32)
    gate_of = jnp.sum(jnp.where(match, all_gates, 0.0), axis=-1)
    rank = exclusive_count(routed)
    slots = jnp.arange(capacity, dtype=jnp.float32)
    pick = (routed[:, None, :] > 0) & (rank[:, None, :] == slots[None, :, None])
    pick_b = pick.astype(jnp.bfloat16)
    inputs = jnp.einsum(
        "srt,stc->src", pick_b, all_tokens, preferred_element_type=jnp.float32
    ).astype(jnp.bfloat16)
    cot_rows = jnp.einsum(
        "srt,stc->src", pick_b, all_cot, preferred_element_type=jnp.float32
    )
    slot_gate = jnp.sum(jnp.where(pick, gate_of[:, None, :], 0.0), axis=-1)
    scaled = (slot_gate[..., None] * cot_rows).astype(jnp.bfloat16)

    weight_pair = gate_up[0]
    weight_down = down_weight[0]
    grad_pair, grad_down, row_grads = expert_backward(
        inputs.reshape(slot_total, model_width),
        scaled.reshape(slot_total, model_width),
        weight_pair,
        weight_down,
    )
    returned = lax.all_to_all(
        row_grads.reshape(expert_count, capacity, model_width),
        "expert",
        split_axis=0,
        concat_axis=0,
        tiled=True,
    )

    own_match = (
        expert_ids[:, :, None] == jnp.arange(expert_count, dtype=jnp.int32)[None, None, :]
    )
    own_routed = jnp.any(own_match, axis=1).astype(jnp.float32)
    own_rank = exclusive_count(own_routed.T).T
    own_pick = (own_routed[:, :, None] > 0) & (
        own_rank[:, :, None] == slots[None, None, :]
    )
    own_pick = own_pick.astype(jnp.bfloat16).reshape(local_tokens, slot_total)
    token_grad = jnp.dot(
        own_pick, returned.reshape(slot_total, model_width), preferred_element_type=jnp.float32
    ).astype(jnp.bfloat16)

    sum_pair, sum_down = (
        lax.psum_scatter(
            grad_pair[None].astype(jnp.bfloat16), "group", scatter_dimension=1, tiled=True
        ).astype(jnp.float32),
        lax.psum_scatter(
            grad_down[None].astype(jnp.bfloat16), "group", scatter_dimension=2, tiled=True
        ).astype(jnp.float32),
    )
    group_index = lax.axis_index("group")
    share_rows = model_width // lax.axis_size("group")
    own_pair = lax.dynamic_slice_in_dim(gate_up, group_index * share_rows, share_rows, 1)
    own_down = lax.dynamic_slice_in_dim(down_weight, group_index * share_rows, share_rows, 2)
    new_pair, first_pair, second_pair = adam_update(
        own_pair, sum_pair, gate_up_moment, gate_up_second
    )
    new_down, first_down, second_down = adam_update(own_down, sum_down, down_moment, down_second)
    full_pair, full_down = (
        lax.all_gather(new_pair, "group", axis=1, tiled=True),
        lax.all_gather(new_down, "group", axis=2, tiled=True),
    )
    return (token_grad, full_pair, full_down, first_pair, second_pair, first_down, second_down)


def solution(mesh):
    rows = P(("group", "expert"), None)
    placed = (
        rows,
        rows,
        rows,
        rows,
        P("expert", None, None),
        P("expert", None, None),
        P("expert", "group", None),
        P("expert", "group", None),
        P("expert", None, "group"),
        P("expert", None, "group"),
    )
    return jax.shard_map(
        local,
        mesh=mesh,
        in_specs=placed,
        out_specs=(
            rows,
            P("expert", None, None),
            P("expert", None, None),
            P("expert", "group", None),
            P("expert", "group", None),
            P("expert", None, "group"),
            P("expert", None, "group"),
        ),
        check_vma=False,
    )
```

```python
import jax
import jax.numpy as jnp
from jax import lax
from jax.sharding import PartitionSpec as P

learn_rate = 0.001
beta_first = 0.9
beta_second = 0.999
adam_eps = 1e-08


def expert_backward(inputs, scaled_parts, weight_gate_up, weight_down):
    hidden_count = weight_down.shape[0]
    width = scaled_parts[0].shape[1]
    projected = jnp.dot(inputs, weight_gate_up, preferred_element_type=jnp.float32)
    gate_part = projected[:, :hidden_count]
    up_part = projected[:, hidden_count:]
    sigmoid_gate = jax.nn.sigmoid(gate_part)
    activated = gate_part * sigmoid_gate
    hidden_act = (activated * up_part).astype(jnp.bfloat16)
    hidden_grad = sum(
        jnp.dot(part, weight_down[:, i * width : (i + 1) * width].T, preferred_element_type=jnp.float32)
        for i, part in enumerate(scaled_parts)
    )
    slope = sigmoid_gate * (1.0 + gate_part * (1.0 - sigmoid_gate))
    hidden_act, up_slope, activated = lax.optimization_barrier(
        (hidden_act, up_part * slope, activated)
    )
    pair_grad = jnp.concatenate(
        [hidden_grad * up_slope, hidden_grad * activated], axis=1
    ).astype(jnp.bfloat16)
    down_grad = jnp.concatenate(
        [jnp.dot(hidden_act.T, part, preferred_element_type=jnp.float32) for part in scaled_parts],
        axis=1,
    )
    gate_up_grad = jnp.dot(inputs.T, pair_grad, preferred_element_type=jnp.float32)
    input_grad = jnp.dot(pair_grad, weight_gate_up.T, preferred_element_type=jnp.float32).astype(
        jnp.bfloat16
    )
    return (gate_up_grad, down_grad, input_grad)


def adam_update(weight, grad, first, second):
    first_new = beta_first * first + (1.0 - beta_first) * grad
    second_new = beta_second * second + (1.0 - beta_second) * grad * grad
    updated = (
        weight.astype(jnp.float32) - learn_rate * first_new / (jnp.sqrt(second_new) + adam_eps)
    ).astype(jnp.bfloat16)
    return (updated, first_new, second_new)


def exclusive_count(flags):
    n = flags.shape[-1]
    earlier = (jnp.arange(n)[:, None] < jnp.arange(n)[None, :]).astype(jnp.bfloat16)
    return jnp.dot(flags.astype(jnp.bfloat16), earlier, preferred_element_type=jnp.float32)


def local(
    tokens,
    cotangent,
    gate_probs,
    expert_ids,
    gate_up,
    down_weight,
    gate_up_moment,
    gate_up_second,
    down_moment,
    down_second,
):
    expert_count = lax.axis_size("expert")
    me = lax.axis_index("expert")
    local_tokens, model_width = tokens.shape
    top_count = expert_ids.shape[1]
    capacity = min(local_tokens, 9 * local_tokens * top_count // (4 * expert_count))
    slot_total = expert_count * capacity

    half_width = model_width // 2
    pieces = []
    rest = gate_probs
    for _ in range(3):
        piece = lax.reduce_precision(rest, exponent_bits=8, mantissa_bits=7)
        pieces.append(piece)
        rest = rest - piece
    meta = jnp.concatenate([expert_ids.astype(jnp.float32)] + pieces, axis=1)
    meta_width = 128
    meta = jnp.pad(meta, ((0, 0), (0, meta_width - meta.shape[1]))).astype(jnp.bfloat16)
    first = lax.all_gather(
        jnp.concatenate([tokens, cotangent[:, :half_width], meta], axis=1), "expert", axis=0
    )
    first, cot_after = lax.optimization_barrier((first, cotangent))
    cot_hi = lax.all_gather(cot_after[:, half_width:], "expert", axis=0)
    meta_at = model_width + half_width
    all_meta = first[..., meta_at : meta_at + 4 * top_count].astype(jnp.float32)
    all_ids = all_meta[..., :top_count].astype(jnp.int32)
    all_gates = (
        all_meta[..., top_count : 2 * top_count] + all_meta[..., 2 * top_count : 3 * top_count]
    ) + all_meta[..., 3 * top_count :]


    match = all_ids == me
    routed = jnp.any(match, axis=-1).astype(jnp.float32)
    gate_of = jnp.sum(jnp.where(match, all_gates, 0.0), axis=-1)
    rank = exclusive_count(routed)
    slots = jnp.arange(capacity, dtype=jnp.float32)
    pick = (routed[:, None, :] > 0) & (rank[:, None, :] == slots[None, :, None])
    pick_b = pick.astype(jnp.bfloat16)
    picked_first = jnp.einsum("srt,stc->src", pick_b, first, preferred_element_type=jnp.float32)
    inputs = picked_first[..., :model_width].astype(jnp.bfloat16)
    picked_first = picked_first[..., : model_width + half_width]
    slot_gate = jnp.sum(jnp.where(pick, gate_of[:, None, :], 0.0), axis=-1)
    picked_hi = jnp.einsum("srt,stc->src", pick_b, cot_hi, preferred_element_type=jnp.float32)
    scaled = [
        (slot_gate[..., None] * part).astype(jnp.bfloat16).reshape(slot_total, half_width)
        for part in (picked_first[..., model_width:], picked_hi)
    ]

    weight_pair = gate_up[0]
    weight_down = down_weight[0]
    grad_pair, grad_down, row_grads = expert_backward(
        inputs.reshape(slot_total, model_width),
        scaled,
        weight_pair,
        weight_down,
    )
    returned = lax.all_to_all(
        row_grads.reshape(expert_count, capacity, model_width),
        "expert",
        split_axis=0,
        concat_axis=0,
        tiled=True,
    )

    own_match = (
        expert_ids[:, :, None] == jnp.arange(expert_count, dtype=jnp.int32)[None, None, :]
    )
    own_routed = jnp.any(own_match, axis=1).astype(jnp.float32)
    own_rank = exclusive_count(own_routed.T).T
    own_pick = (own_routed[:, :, None] > 0) & (
        own_rank[:, :, None] == slots[None, None, :]
    )
    own_pick = own_pick.astype(jnp.bfloat16).reshape(local_tokens, slot_total)
    token_grad = jnp.dot(
        own_pick, returned.reshape(slot_total, model_width), preferred_element_type=jnp.float32
    ).astype(jnp.bfloat16)

    sum_pair, sum_down = (
        lax.psum_scatter(
            grad_pair[None].astype(jnp.bfloat16), "group", scatter_dimension=1, tiled=True
        ).astype(jnp.float32),
        lax.psum_scatter(
            grad_down[None].astype(jnp.bfloat16), "group", scatter_dimension=2, tiled=True
        ).astype(jnp.float32),
    )
    group_index = lax.axis_index("group")
    share_rows = model_width // lax.axis_size("group")
    own_pair = lax.dynamic_slice_in_dim(gate_up, group_index * share_rows, share_rows, 1)
    own_down = lax.dynamic_slice_in_dim(down_weight, group_index * share_rows, share_rows, 2)
    new_pair, first_pair, second_pair = adam_update(
        own_pair, sum_pair, gate_up_moment, gate_up_second
    )
    new_down, first_down, second_down = adam_update(own_down, sum_down, down_moment, down_second)
    full_pair, full_down = (
        lax.all_gather(new_pair, "group", axis=1, tiled=True),
        lax.all_gather(new_down, "group", axis=2, tiled=True),
    )
    return (token_grad, full_pair, full_down, first_pair, second_pair, first_down, second_down)


def solution(mesh):
    rows = P(("group", "expert"), None)
    placed = (
        rows,
        rows,
        rows,
        rows,
        P("expert", None, None),
        P("expert", None, None),
        P("expert", "group", None),
        P("expert", "group", None),
        P("expert", None, "group"),
        P("expert", None, "group"),
    )
    return jax.shard_map(
        local,
        mesh=mesh,
        in_specs=placed,
        out_specs=(
            rows,
            P("expert", None, None),
            P("expert", None, None),
            P("expert", "group", None),
            P("expert", "group", None),
            P("expert", None, "group"),
            P("expert", None, "group"),
        ),
        check_vma=False,
    )
```

```python
import jax
import jax.numpy as jnp
from jax import lax
from jax.sharding import PartitionSpec as P

learn_rate = 0.001
beta_first = 0.9
beta_second = 0.999
adam_eps = 1e-08


def expert_backward(inputs, scaled_parts, weight_gate_up, weight_down):
    hidden_count = weight_down.shape[0]
    width = scaled_parts[0].shape[1]
    projected = jnp.dot(inputs, weight_gate_up, preferred_element_type=jnp.float32)
    gate_part = projected[:, :hidden_count]
    up_part = projected[:, hidden_count:]
    sigmoid_gate = jax.nn.sigmoid(gate_part)
    activated = gate_part * sigmoid_gate
    hidden_act = (activated * up_part).astype(jnp.bfloat16)
    hidden_grad = sum(
        jnp.dot(part, weight_down[:, i * width : (i + 1) * width].T, preferred_element_type=jnp.float32)
        for i, part in enumerate(scaled_parts)
    )
    slope = sigmoid_gate * (1.0 + gate_part * (1.0 - sigmoid_gate))
    hidden_act, up_slope, activated = lax.optimization_barrier(
        (hidden_act, up_part * slope, activated)
    )
    pair_grad = jnp.concatenate(
        [hidden_grad * up_slope, hidden_grad * activated], axis=1
    ).astype(jnp.bfloat16)
    down_grad = jnp.concatenate(
        [jnp.dot(hidden_act.T, part, preferred_element_type=jnp.float32) for part in scaled_parts],
        axis=1,
    )
    gate_up_grad = jnp.dot(inputs.T, pair_grad, preferred_element_type=jnp.float32)
    input_grad = jnp.dot(pair_grad, weight_gate_up.T, preferred_element_type=jnp.float32).astype(
        jnp.bfloat16
    )
    return (gate_up_grad, down_grad, input_grad)


def adam_update(weight, grad, first, second):
    first_new = beta_first * first + (1.0 - beta_first) * grad
    second_new = beta_second * second + (1.0 - beta_second) * grad * grad
    updated = (
        weight.astype(jnp.float32) - learn_rate * first_new / (jnp.sqrt(second_new) + adam_eps)
    ).astype(jnp.bfloat16)
    return (updated, first_new, second_new)


def exclusive_count(flags):
    n = flags.shape[-1]
    earlier = (jnp.arange(n)[:, None] < jnp.arange(n)[None, :]).astype(jnp.bfloat16)
    return jnp.dot(flags.astype(jnp.bfloat16), earlier, preferred_element_type=jnp.float32)


def local(
    tokens,
    cotangent,
    gate_probs,
    expert_ids,
    gate_up,
    down_weight,
    gate_up_moment,
    gate_up_second,
    down_moment,
    down_second,
):
    expert_count = lax.axis_size("expert")
    me = lax.axis_index("expert")
    local_tokens, model_width = tokens.shape
    top_count = expert_ids.shape[1]
    capacity = min(local_tokens, 9 * local_tokens * top_count // (4 * expert_count))
    slot_total = expert_count * capacity

    half_width = model_width // 2
    pieces = []
    rest = gate_probs
    for _ in range(3):
        piece = lax.reduce_precision(rest, exponent_bits=8, mantissa_bits=7)
        pieces.append(piece)
        rest = rest - piece
    meta = jnp.concatenate([expert_ids.astype(jnp.float32)] + pieces, axis=1)
    meta_width = 128
    meta = jnp.pad(meta, ((0, 0), (0, meta_width - meta.shape[1]))).astype(jnp.bfloat16)
    first = lax.all_gather(
        jnp.concatenate([tokens, cotangent[:, :half_width], meta], axis=1), "expert", axis=0
    )
    first, cot_after = lax.optimization_barrier((first, cotangent))
    cot_hi = lax.all_gather(cot_after[:, half_width:], "expert", axis=0)
    meta_at = model_width + half_width
    all_meta = first[..., meta_at : meta_at + 4 * top_count].astype(jnp.float32)
    all_ids = all_meta[..., :top_count].astype(jnp.int32)
    all_gates = (
        all_meta[..., top_count : 2 * top_count] + all_meta[..., 2 * top_count : 3 * top_count]
    ) + all_meta[..., 3 * top_count :]


    match = all_ids == me
    routed = jnp.any(match, axis=-1).astype(jnp.float32)
    gate_of = jnp.sum(jnp.where(match, all_gates, 0.0), axis=-1)
    rank = exclusive_count(routed)
    slots = jnp.arange(capacity, dtype=jnp.float32)
    pick = (routed[:, None, :] > 0) & (rank[:, None, :] == slots[None, :, None])
    pick_b = pick.astype(jnp.bfloat16)
    picked_first = jnp.einsum(
        "srt,stc->src", pick_b, first, preferred_element_type=jnp.float32
    ).astype(jnp.bfloat16)
    inputs = picked_first[..., :model_width]
    slot_gate = jnp.sum(jnp.where(pick, gate_of[:, None, :], 0.0), axis=-1)
    picked_hi = jnp.einsum(
        "srt,stc->src", pick_b, cot_hi, preferred_element_type=jnp.float32
    ).astype(jnp.bfloat16)
    scaled = [
        (slot_gate[..., None] * part.astype(jnp.float32))
        .astype(jnp.bfloat16)
        .reshape(slot_total, half_width)
        for part in (picked_first[..., model_width:meta_at], picked_hi)
    ]

    weight_pair = gate_up[0]
    weight_down = down_weight[0]
    grad_pair, grad_down, row_grads = expert_backward(
        inputs.reshape(slot_total, model_width),
        scaled,
        weight_pair,
        weight_down,
    )
    returned = lax.all_to_all(
        row_grads.reshape(expert_count, capacity, model_width),
        "expert",
        split_axis=0,
        concat_axis=0,
        tiled=True,
    )

    own_match = (
        expert_ids[:, :, None] == jnp.arange(expert_count, dtype=jnp.int32)[None, None, :]
    )
    own_routed = jnp.any(own_match, axis=1).astype(jnp.float32)
    own_rank = exclusive_count(own_routed.T).T
    own_pick = (own_routed[:, :, None] > 0) & (
        own_rank[:, :, None] == slots[None, None, :]
    )
    own_pick = own_pick.astype(jnp.bfloat16).reshape(local_tokens, slot_total)
    token_grad = jnp.dot(
        own_pick, returned.reshape(slot_total, model_width), preferred_element_type=jnp.float32
    ).astype(jnp.bfloat16)

    sum_pair, sum_down = (
        lax.psum_scatter(
            grad_pair[None].astype(jnp.bfloat16), "group", scatter_dimension=1, tiled=True
        ).astype(jnp.float32),
        lax.psum_scatter(
            grad_down[None].astype(jnp.bfloat16), "group", scatter_dimension=2, tiled=True
        ).astype(jnp.float32),
    )
    group_index = lax.axis_index("group")
    share_rows = model_width // lax.axis_size("group")
    own_pair = lax.dynamic_slice_in_dim(gate_up, group_index * share_rows, share_rows, 1)
    own_down = lax.dynamic_slice_in_dim(down_weight, group_index * share_rows, share_rows, 2)
    new_pair, first_pair, second_pair = adam_update(
        own_pair, sum_pair, gate_up_moment, gate_up_second
    )
    new_down, first_down, second_down = adam_update(own_down, sum_down, down_moment, down_second)
    full_pair, full_down = (
        lax.all_gather(new_pair, "group", axis=1, tiled=True),
        lax.all_gather(new_down, "group", axis=2, tiled=True),
    )
    return (token_grad, full_pair, full_down, first_pair, second_pair, first_down, second_down)


def solution(mesh):
    rows = P(("group", "expert"), None)
    placed = (
        rows,
        rows,
        rows,
        rows,
        P("expert", None, None),
        P("expert", None, None),
        P("expert", "group", None),
        P("expert", "group", None),
        P("expert", None, "group"),
        P("expert", None, "group"),
    )
    return jax.shard_map(
        local,
        mesh=mesh,
        in_specs=placed,
        out_specs=(
            rows,
            P("expert", None, None),
            P("expert", None, None),
            P("expert", "group", None),
            P("expert", "group", None),
            P("expert", None, "group"),
            P("expert", None, "group"),
        ),
        check_vma=False,
    )
```

```python
import jax
import jax.numpy as jnp
from jax import lax
from jax.sharding import PartitionSpec as P

learn_rate = 0.001
beta_first = 0.9
beta_second = 0.999
adam_eps = 1e-08


def expert_backward(inputs, scaled_parts, weight_gate_up, weight_down):
    hidden_count = weight_down.shape[0]
    width = scaled_parts[0].shape[1]
    projected = jnp.dot(inputs, weight_gate_up, preferred_element_type=jnp.float32)
    gate_part = projected[:, :hidden_count]
    up_part = projected[:, hidden_count:]
    sigmoid_gate = jax.nn.sigmoid(gate_part)
    activated = gate_part * sigmoid_gate
    hidden_act = (activated * up_part).astype(jnp.bfloat16)
    hidden_grad = sum(
        jnp.dot(part, weight_down[:, i * width : (i + 1) * width].T, preferred_element_type=jnp.float32)
        for i, part in enumerate(scaled_parts)
    )
    slope = sigmoid_gate * (1.0 + gate_part * (1.0 - sigmoid_gate))
    hidden_act, up_slope, activated = lax.optimization_barrier(
        (hidden_act, up_part * slope, activated)
    )
    pair_grad = jnp.concatenate(
        [hidden_grad * up_slope, hidden_grad * activated], axis=1
    ).astype(jnp.bfloat16)
    down_grad = jnp.concatenate(
        [jnp.dot(hidden_act.T, part, preferred_element_type=jnp.float32) for part in scaled_parts],
        axis=1,
    )
    gate_up_grad = jnp.dot(inputs.T, pair_grad, preferred_element_type=jnp.float32)
    input_grad = jnp.dot(pair_grad, weight_gate_up.T, preferred_element_type=jnp.float32).astype(
        jnp.bfloat16
    )
    return (gate_up_grad, down_grad, input_grad)


def adam_update(weight, grad, first, second):
    first_new = beta_first * first + (1.0 - beta_first) * grad
    second_new = beta_second * second + (1.0 - beta_second) * grad * grad
    updated = (
        weight.astype(jnp.float32) - learn_rate * first_new / (jnp.sqrt(second_new) + adam_eps)
    ).astype(jnp.bfloat16)
    return (updated, first_new, second_new)


def exclusive_count(flags):
    n = flags.shape[-1]
    earlier = (jnp.arange(n)[:, None] < jnp.arange(n)[None, :]).astype(jnp.bfloat16)
    return jnp.dot(flags.astype(jnp.bfloat16), earlier, preferred_element_type=jnp.float32)


def local(
    tokens,
    cotangent,
    gate_probs,
    expert_ids,
    gate_up,
    down_weight,
    gate_up_moment,
    gate_up_second,
    down_moment,
    down_second,
):
    expert_count = lax.axis_size("expert")
    me = lax.axis_index("expert")
    local_tokens, model_width = tokens.shape
    top_count = expert_ids.shape[1]
    capacity = min(local_tokens, 9 * local_tokens * top_count // (4 * expert_count))
    slot_total = expert_count * capacity

    half_width = model_width // 2
    pieces = []
    rest = gate_probs
    for _ in range(3):
        piece = lax.reduce_precision(rest, exponent_bits=8, mantissa_bits=7)
        pieces.append(piece)
        rest = rest - piece
    meta = jnp.concatenate([expert_ids.astype(jnp.float32)] + pieces, axis=1)
    meta_width = 128
    meta = jnp.pad(meta, ((0, 0), (0, meta_width - meta.shape[1]))).astype(jnp.bfloat16)
    first = lax.all_gather(
        jnp.concatenate([tokens, cotangent[:, :half_width], meta], axis=1), "expert", axis=0
    )
    first, cot_after = lax.optimization_barrier((first, cotangent))
    cot_hi = lax.all_gather(cot_after[:, half_width:], "expert", axis=0)
    meta_at = model_width + half_width
    all_meta = first[..., meta_at : meta_at + 4 * top_count].astype(jnp.float32)
    all_ids = all_meta[..., :top_count].astype(jnp.int32)
    all_gates = (
        all_meta[..., top_count : 2 * top_count] + all_meta[..., 2 * top_count : 3 * top_count]
    ) + all_meta[..., 3 * top_count :]


    match = all_ids == me
    routed = jnp.any(match, axis=-1).astype(jnp.float32)
    gate_of = jnp.sum(jnp.where(match, all_gates, 0.0), axis=-1)
    rank = exclusive_count(routed)
    slots = jnp.arange(capacity, dtype=jnp.float32)
    pick = (routed[:, None, :] > 0) & (rank[:, None, :] == slots[None, :, None])
    pick_b = pick.astype(jnp.bfloat16)
    inputs = jnp.einsum(
        "srt,stc->src", pick_b, first[..., :model_width], preferred_element_type=jnp.float32
    ).astype(jnp.bfloat16)
    picked_lo = jnp.einsum(
        "srt,stc->src", pick_b, first[..., model_width:meta_at], preferred_element_type=jnp.float32
    ).astype(jnp.bfloat16)
    slot_gate = jnp.sum(jnp.where(pick, gate_of[:, None, :], 0.0), axis=-1)
    picked_hi = jnp.einsum(
        "srt,stc->src", pick_b, cot_hi, preferred_element_type=jnp.float32
    ).astype(jnp.bfloat16)
    scaled = [
        (slot_gate[..., None] * part.astype(jnp.float32))
        .astype(jnp.bfloat16)
        .reshape(slot_total, half_width)
        for part in (picked_lo, picked_hi)
    ]

    weight_pair = gate_up[0]
    weight_down = down_weight[0]
    grad_pair, grad_down, row_grads = expert_backward(
        inputs.reshape(slot_total, model_width),
        scaled,
        weight_pair,
        weight_down,
    )
    returned = lax.all_to_all(
        row_grads.reshape(expert_count, capacity, model_width),
        "expert",
        split_axis=0,
        concat_axis=0,
        tiled=True,
    )

    own_match = (
        expert_ids[:, :, None] == jnp.arange(expert_count, dtype=jnp.int32)[None, None, :]
    )
    own_routed = jnp.any(own_match, axis=1).astype(jnp.float32)
    own_rank = exclusive_count(own_routed.T).T
    own_pick = (own_routed[:, :, None] > 0) & (
        own_rank[:, :, None] == slots[None, None, :]
    )
    own_pick = own_pick.astype(jnp.bfloat16).reshape(local_tokens, slot_total)
    token_grad = jnp.dot(
        own_pick, returned.reshape(slot_total, model_width), preferred_element_type=jnp.float32
    ).astype(jnp.bfloat16)

    sum_pair, sum_down = (
        lax.psum_scatter(
            grad_pair[None].astype(jnp.bfloat16), "group", scatter_dimension=1, tiled=True
        ).astype(jnp.float32),
        lax.psum_scatter(
            grad_down[None].astype(jnp.bfloat16), "group", scatter_dimension=2, tiled=True
        ).astype(jnp.float32),
    )
    group_index = lax.axis_index("group")
    share_rows = model_width // lax.axis_size("group")
    own_pair = lax.dynamic_slice_in_dim(gate_up, group_index * share_rows, share_rows, 1)
    own_down = lax.dynamic_slice_in_dim(down_weight, group_index * share_rows, share_rows, 2)
    new_pair, first_pair, second_pair = adam_update(
        own_pair, sum_pair, gate_up_moment, gate_up_second
    )
    new_down, first_down, second_down = adam_update(own_down, sum_down, down_moment, down_second)
    full_pair, full_down = (
        lax.all_gather(new_pair, "group", axis=1, tiled=True),
        lax.all_gather(new_down, "group", axis=2, tiled=True),
    )
    return (token_grad, full_pair, full_down, first_pair, second_pair, first_down, second_down)


def solution(mesh):
    rows = P(("group", "expert"), None)
    placed = (
        rows,
        rows,
        rows,
        rows,
        P("expert", None, None),
        P("expert", None, None),
        P("expert", "group", None),
        P("expert", "group", None),
        P("expert", None, "group"),
        P("expert", None, "group"),
    )
    return jax.shard_map(
        local,
        mesh=mesh,
        in_specs=placed,
        out_specs=(
            rows,
            P("expert", None, None),
            P("expert", None, None),
            P("expert", "group", None),
            P("expert", "group", None),
            P("expert", None, "group"),
            P("expert", None, "group"),
        ),
        check_vma=False,
    )
```

```python
import jax
import jax.numpy as jnp
from jax import lax
from jax.sharding import PartitionSpec as P

learn_rate = 0.001
beta_first = 0.9
beta_second = 0.999
adam_eps = 1e-08


def expert_backward(inputs, scaled_parts, weight_gate_up, weight_down):
    hidden_count = weight_down.shape[0]
    offsets = [0]
    for part in scaled_parts:
        offsets.append(offsets[-1] + part.shape[1])
    projected = jnp.dot(inputs, weight_gate_up, preferred_element_type=jnp.float32)
    gate_part = projected[:, :hidden_count]
    up_part = projected[:, hidden_count:]
    sigmoid_gate = jax.nn.sigmoid(gate_part)
    activated = gate_part * sigmoid_gate
    hidden_act = (activated * up_part).astype(jnp.bfloat16)
    hidden_grad = sum(
        jnp.dot(part, weight_down[:, offsets[i] : offsets[i + 1]].T, preferred_element_type=jnp.float32)
        for i, part in enumerate(scaled_parts)
    )
    slope = sigmoid_gate * (1.0 + gate_part * (1.0 - sigmoid_gate))
    hidden_act, up_slope, activated = lax.optimization_barrier(
        (hidden_act, up_part * slope, activated)
    )
    pair_grad = jnp.concatenate(
        [hidden_grad * up_slope, hidden_grad * activated], axis=1
    ).astype(jnp.bfloat16)
    down_grad = jnp.concatenate(
        [jnp.dot(hidden_act.T, part, preferred_element_type=jnp.float32) for part in scaled_parts],
        axis=1,
    )
    gate_up_grad = jnp.dot(inputs.T, pair_grad, preferred_element_type=jnp.float32)
    input_grad = jnp.dot(pair_grad, weight_gate_up.T, preferred_element_type=jnp.float32).astype(
        jnp.bfloat16
    )
    return (gate_up_grad, down_grad, input_grad)


def adam_update(weight, grad, first, second):
    first_new = beta_first * first + (1.0 - beta_first) * grad
    second_new = beta_second * second + (1.0 - beta_second) * grad * grad
    updated = (
        weight.astype(jnp.float32) - learn_rate * first_new / (jnp.sqrt(second_new) + adam_eps)
    ).astype(jnp.bfloat16)
    return (updated, first_new, second_new)


def exclusive_count(flags):
    n = flags.shape[-1]
    earlier = (jnp.arange(n)[:, None] < jnp.arange(n)[None, :]).astype(jnp.bfloat16)
    return jnp.dot(flags.astype(jnp.bfloat16), earlier, preferred_element_type=jnp.float32)


def local(
    tokens,
    cotangent,
    gate_probs,
    expert_ids,
    gate_up,
    down_weight,
    gate_up_moment,
    gate_up_second,
    down_moment,
    down_second,
):
    expert_count = lax.axis_size("expert")
    me = lax.axis_index("expert")
    local_tokens, model_width = tokens.shape
    top_count = expert_ids.shape[1]
    capacity = min(local_tokens, 9 * local_tokens * top_count // (4 * expert_count))
    slot_total = expert_count * capacity

    half_width = model_width * 3 // 4
    pieces = []
    rest = gate_probs
    for _ in range(3):
        piece = lax.reduce_precision(rest, exponent_bits=8, mantissa_bits=7)
        pieces.append(piece)
        rest = rest - piece
    meta = jnp.concatenate([expert_ids.astype(jnp.float32)] + pieces, axis=1)
    meta_width = 128
    meta = jnp.pad(meta, ((0, 0), (0, meta_width - meta.shape[1]))).astype(jnp.bfloat16)
    first = lax.all_gather(
        jnp.concatenate([tokens, cotangent[:, :half_width], meta], axis=1), "expert", axis=0
    )
    first, cot_after = lax.optimization_barrier((first, cotangent))
    cot_hi = lax.all_gather(cot_after[:, half_width:], "expert", axis=0)
    meta_at = model_width + half_width
    all_meta = first[..., meta_at : meta_at + 4 * top_count].astype(jnp.float32)
    all_ids = all_meta[..., :top_count].astype(jnp.int32)
    all_gates = (
        all_meta[..., top_count : 2 * top_count] + all_meta[..., 2 * top_count : 3 * top_count]
    ) + all_meta[..., 3 * top_count :]


    match = all_ids == me
    routed = jnp.any(match, axis=-1).astype(jnp.float32)
    gate_of = jnp.sum(jnp.where(match, all_gates, 0.0), axis=-1)
    rank = exclusive_count(routed)
    slots = jnp.arange(capacity, dtype=jnp.float32)
    pick = (routed[:, None, :] > 0) & (rank[:, None, :] == slots[None, :, None])
    pick_b = pick.astype(jnp.bfloat16)
    inputs = jnp.einsum(
        "srt,stc->src", pick_b, first[..., :model_width], preferred_element_type=jnp.float32
    ).astype(jnp.bfloat16)
    picked_lo = jnp.einsum(
        "srt,stc->src", pick_b, first[..., model_width:meta_at], preferred_element_type=jnp.float32
    ).astype(jnp.bfloat16)
    slot_gate = jnp.sum(jnp.where(pick, gate_of[:, None, :], 0.0), axis=-1)
    picked_hi = jnp.einsum(
        "srt,stc->src", pick_b, cot_hi, preferred_element_type=jnp.float32
    ).astype(jnp.bfloat16)
    scaled = [
        (slot_gate[..., None] * part.astype(jnp.float32))
        .astype(jnp.bfloat16)
        .reshape(slot_total, part.shape[-1])
        for part in (picked_lo, picked_hi)
    ]

    weight_pair = gate_up[0]
    weight_down = down_weight[0]
    grad_pair, grad_down, row_grads = expert_backward(
        inputs.reshape(slot_total, model_width),
        scaled,
        weight_pair,
        weight_down,
    )
    returned = lax.all_to_all(
        row_grads.reshape(expert_count, capacity, model_width),
        "expert",
        split_axis=0,
        concat_axis=0,
        tiled=True,
    )

    own_match = (
        expert_ids[:, :, None] == jnp.arange(expert_count, dtype=jnp.int32)[None, None, :]
    )
    own_routed = jnp.any(own_match, axis=1).astype(jnp.float32)
    own_rank = exclusive_count(own_routed.T).T
    own_pick = (own_routed[:, :, None] > 0) & (
        own_rank[:, :, None] == slots[None, None, :]
    )
    own_pick = own_pick.astype(jnp.bfloat16).reshape(local_tokens, slot_total)
    token_grad = jnp.dot(
        own_pick, returned.reshape(slot_total, model_width), preferred_element_type=jnp.float32
    ).astype(jnp.bfloat16)

    sum_pair, sum_down = (
        lax.psum_scatter(
            grad_pair[None].astype(jnp.bfloat16), "group", scatter_dimension=1, tiled=True
        ).astype(jnp.float32),
        lax.psum_scatter(
            grad_down[None].astype(jnp.bfloat16), "group", scatter_dimension=2, tiled=True
        ).astype(jnp.float32),
    )
    group_index = lax.axis_index("group")
    share_rows = model_width // lax.axis_size("group")
    own_pair = lax.dynamic_slice_in_dim(gate_up, group_index * share_rows, share_rows, 1)
    own_down = lax.dynamic_slice_in_dim(down_weight, group_index * share_rows, share_rows, 2)
    new_pair, first_pair, second_pair = adam_update(
        own_pair, sum_pair, gate_up_moment, gate_up_second
    )
    new_down, first_down, second_down = adam_update(own_down, sum_down, down_moment, down_second)
    full_pair, full_down = (
        lax.all_gather(new_pair, "group", axis=1, tiled=True),
        lax.all_gather(new_down, "group", axis=2, tiled=True),
    )
    return (token_grad, full_pair, full_down, first_pair, second_pair, first_down, second_down)


def solution(mesh):
    rows = P(("group", "expert"), None)
    placed = (
        rows,
        rows,
        rows,
        rows,
        P("expert", None, None),
        P("expert", None, None),
        P("expert", "group", None),
        P("expert", "group", None),
        P("expert", None, "group"),
        P("expert", None, "group"),
    )
    return jax.shard_map(
        local,
        mesh=mesh,
        in_specs=placed,
        out_specs=(
            rows,
            P("expert", None, None),
            P("expert", None, None),
            P("expert", "group", None),
            P("expert", "group", None),
            P("expert", None, "group"),
            P("expert", None, "group"),
        ),
        check_vma=False,
    )
```

```python
import jax
import jax.numpy as jnp
from jax import lax
from jax.sharding import PartitionSpec as P

learn_rate = 0.001
beta_first = 0.9
beta_second = 0.999
adam_eps = 1e-08


def expert_backward(inputs, scaled_parts, weight_gate_up, weight_down):
    hidden_count = weight_down.shape[0]
    width = scaled_parts[0].shape[1]
    projected = jnp.dot(inputs, weight_gate_up, preferred_element_type=jnp.float32)
    gate_part = projected[:, :hidden_count]
    up_part = projected[:, hidden_count:]
    sigmoid_gate = jax.nn.sigmoid(gate_part)
    activated = gate_part * sigmoid_gate
    hidden_act = (activated * up_part).astype(jnp.bfloat16)
    hidden_grad = sum(
        jnp.dot(part, weight_down[:, i * width : (i + 1) * width].T, preferred_element_type=jnp.float32)
        for i, part in enumerate(scaled_parts)
    )
    slope = sigmoid_gate * (1.0 + gate_part * (1.0 - sigmoid_gate))
    hidden_act, up_slope, activated = lax.optimization_barrier(
        (hidden_act, up_part * slope, activated)
    )
    pair_grad = jnp.concatenate(
        [hidden_grad * up_slope, hidden_grad * activated], axis=1
    ).astype(jnp.bfloat16)
    down_grad = jnp.concatenate(
        [jnp.dot(hidden_act.T, part, preferred_element_type=jnp.float32) for part in scaled_parts],
        axis=1,
    )
    gate_up_grad = jnp.dot(inputs.T, pair_grad, preferred_element_type=jnp.float32)
    input_grad = jnp.dot(pair_grad, weight_gate_up.T, preferred_element_type=jnp.float32).astype(
        jnp.bfloat16
    )
    return (gate_up_grad, down_grad, input_grad)


def adam_update(weight, grad, first, second):
    first_new = beta_first * first + (1.0 - beta_first) * grad
    second_new = beta_second * second + (1.0 - beta_second) * grad * grad
    updated = (
        weight.astype(jnp.float32) - learn_rate * first_new / (jnp.sqrt(second_new) + adam_eps)
    ).astype(jnp.bfloat16)
    return (updated, first_new, second_new)


def exclusive_count(flags):
    n = flags.shape[-1]
    earlier = (jnp.arange(n)[:, None] < jnp.arange(n)[None, :]).astype(jnp.bfloat16)
    return jnp.dot(flags.astype(jnp.bfloat16), earlier, preferred_element_type=jnp.float32)


def local(
    tokens,
    cotangent,
    gate_probs,
    expert_ids,
    gate_up,
    down_weight,
    gate_up_moment,
    gate_up_second,
    down_moment,
    down_second,
):
    expert_count = lax.axis_size("expert")
    me = lax.axis_index("expert")
    local_tokens, model_width = tokens.shape
    top_count = expert_ids.shape[1]
    capacity = min(local_tokens, 9 * local_tokens * top_count // (4 * expert_count))
    slot_total = expert_count * capacity

    half_width = model_width // 2
    pieces = []
    rest = gate_probs
    for _ in range(3):
        piece = lax.reduce_precision(rest, exponent_bits=8, mantissa_bits=7)
        pieces.append(piece)
        rest = rest - piece
    meta = jnp.concatenate([expert_ids.astype(jnp.float32)] + pieces, axis=1)
    meta_width = 128
    meta = jnp.pad(meta, ((0, 0), (0, meta_width - meta.shape[1]))).astype(jnp.bfloat16)
    first = lax.all_gather(
        jnp.concatenate([tokens, cotangent[:, :half_width], meta], axis=1), "expert", axis=0
    )
    first, cot_after = lax.optimization_barrier((first, cotangent))
    cot_hi = lax.all_gather(cot_after[:, half_width:], "expert", axis=0)
    meta_at = model_width + half_width
    all_meta = first[..., meta_at : meta_at + 4 * top_count].astype(jnp.float32)
    all_ids = all_meta[..., :top_count].astype(jnp.int32)
    all_gates = (
        all_meta[..., top_count : 2 * top_count] + all_meta[..., 2 * top_count : 3 * top_count]
    ) + all_meta[..., 3 * top_count :]


    match = all_ids == me
    routed = jnp.any(match, axis=-1).astype(jnp.float32)
    gate_of = jnp.sum(jnp.where(match, all_gates, 0.0), axis=-1)
    rank = exclusive_count(routed)
    slots = jnp.arange(capacity, dtype=jnp.float32)
    pick = (routed[:, None, :] > 0) & (rank[:, None, :] == slots[None, :, None])
    pick_b = pick.astype(jnp.bfloat16)
    picked_first = jnp.einsum(
        "srt,stc->src", pick_b, first, preferred_element_type=jnp.float32
    ).astype(jnp.bfloat16)
    inputs = picked_first[..., :model_width]
    slot_gate = jnp.sum(jnp.where(pick, gate_of[:, None, :], 0.0), axis=-1)
    picked_hi = jnp.einsum(
        "srt,stc->src", pick_b, cot_hi, preferred_element_type=jnp.float32
    ).astype(jnp.bfloat16)
    scaled = [
        (slot_gate[..., None] * part.astype(jnp.float32))
        .astype(jnp.bfloat16)
        .reshape(slot_total, half_width)
        for part in (picked_first[..., model_width:meta_at], picked_hi)
    ]

    weight_pair = gate_up[0]
    weight_down = down_weight[0]
    grad_pair, grad_down, row_grads = expert_backward(
        inputs.reshape(slot_total, model_width),
        scaled,
        weight_pair,
        weight_down,
    )
    rolled = jnp.roll(row_grads.reshape(expert_count, capacity, model_width), -me, axis=0)
    arrived = [rolled[0]]
    for shift in range(1, expert_count):
        pairs = [(i, (i + shift) % expert_count) for i in range(expert_count)]
        arrived.append(lax.ppermute(rolled[shift], "expert", pairs))
    returned = jnp.stack(arrived)
    expert_of = (me - jnp.arange(expert_count, dtype=jnp.int32)) % expert_count

    own_match = expert_ids[:, :, None] == expert_of[None, None, :]
    own_routed = jnp.any(own_match, axis=1).astype(jnp.float32)
    own_rank = exclusive_count(own_routed.T).T
    own_pick = (own_routed[:, :, None] > 0) & (
        own_rank[:, :, None] == slots[None, None, :]
    )
    own_pick = own_pick.astype(jnp.bfloat16).reshape(local_tokens, slot_total)
    token_grad = jnp.dot(
        own_pick, returned.reshape(slot_total, model_width), preferred_element_type=jnp.float32
    ).astype(jnp.bfloat16)

    sum_pair, sum_down = (
        lax.psum_scatter(
            grad_pair[None].astype(jnp.bfloat16), "group", scatter_dimension=1, tiled=True
        ).astype(jnp.float32),
        lax.psum_scatter(
            grad_down[None].astype(jnp.bfloat16), "group", scatter_dimension=2, tiled=True
        ).astype(jnp.float32),
    )
    group_index = lax.axis_index("group")
    share_rows = model_width // lax.axis_size("group")
    own_pair = lax.dynamic_slice_in_dim(gate_up, group_index * share_rows, share_rows, 1)
    own_down = lax.dynamic_slice_in_dim(down_weight, group_index * share_rows, share_rows, 2)
    new_pair, first_pair, second_pair = adam_update(
        own_pair, sum_pair, gate_up_moment, gate_up_second
    )
    new_down, first_down, second_down = adam_update(own_down, sum_down, down_moment, down_second)
    full_pair, full_down = (
        lax.all_gather(new_pair, "group", axis=1, tiled=True),
        lax.all_gather(new_down, "group", axis=2, tiled=True),
    )
    return (token_grad, full_pair, full_down, first_pair, second_pair, first_down, second_down)


def solution(mesh):
    rows = P(("group", "expert"), None)
    placed = (
        rows,
        rows,
        rows,
        rows,
        P("expert", None, None),
        P("expert", None, None),
        P("expert", "group", None),
        P("expert", "group", None),
        P("expert", None, "group"),
        P("expert", None, "group"),
    )
    return jax.shard_map(
        local,
        mesh=mesh,
        in_specs=placed,
        out_specs=(
            rows,
            P("expert", None, None),
            P("expert", None, None),
            P("expert", "group", None),
            P("expert", "group", None),
            P("expert", None, "group"),
            P("expert", None, "group"),
        ),
        check_vma=False,
    )
```

```python
import jax
import jax.numpy as jnp
from jax import lax
from jax.sharding import PartitionSpec as P

learn_rate = 0.001
beta_first = 0.9
beta_second = 0.999
adam_eps = 1e-08


def expert_backward(inputs, scaled_parts, weight_gate_up, weight_down):
    hidden_count = weight_down.shape[0]
    width = scaled_parts[0].shape[1]
    projected = jnp.dot(inputs, weight_gate_up, preferred_element_type=jnp.float32)
    gate_part = projected[:, :hidden_count]
    up_part = projected[:, hidden_count:]
    sigmoid_gate = jax.nn.sigmoid(gate_part)
    activated = gate_part * sigmoid_gate
    hidden_act = (activated * up_part).astype(jnp.bfloat16)
    hidden_grad = sum(
        jnp.dot(part, weight_down[:, i * width : (i + 1) * width].T, preferred_element_type=jnp.float32)
        for i, part in enumerate(scaled_parts)
    )
    slope = sigmoid_gate * (1.0 + gate_part * (1.0 - sigmoid_gate))
    hidden_act, up_slope, activated = lax.optimization_barrier(
        (hidden_act, up_part * slope, activated)
    )
    pair_grad = jnp.concatenate(
        [hidden_grad * up_slope, hidden_grad * activated], axis=1
    ).astype(jnp.bfloat16)
    down_grad = jnp.concatenate(
        [jnp.dot(hidden_act.T, part, preferred_element_type=jnp.float32) for part in scaled_parts],
        axis=1,
    )
    gate_up_grad = jnp.dot(inputs.T, pair_grad, preferred_element_type=jnp.float32)
    input_grad = jnp.dot(pair_grad, weight_gate_up.T, preferred_element_type=jnp.float32).astype(
        jnp.bfloat16
    )
    return (gate_up_grad, down_grad, input_grad)


def adam_update(weight, grad, first, second):
    first_new = beta_first * first + (1.0 - beta_first) * grad
    second_new = beta_second * second + (1.0 - beta_second) * grad * grad
    updated = (
        weight.astype(jnp.float32) - learn_rate * first_new / (jnp.sqrt(second_new) + adam_eps)
    ).astype(jnp.bfloat16)
    return (updated, first_new, second_new)


def exclusive_count(flags):
    n = flags.shape[-1]
    earlier = (jnp.arange(n)[:, None] < jnp.arange(n)[None, :]).astype(jnp.bfloat16)
    return jnp.dot(flags.astype(jnp.bfloat16), earlier, preferred_element_type=jnp.float32)


def local(
    tokens,
    cotangent,
    gate_probs,
    expert_ids,
    gate_up,
    down_weight,
    gate_up_moment,
    gate_up_second,
    down_moment,
    down_second,
):
    expert_count = lax.axis_size("expert")
    me = lax.axis_index("expert")
    local_tokens, model_width = tokens.shape
    top_count = expert_ids.shape[1]
    capacity = min(local_tokens, 9 * local_tokens * top_count // (4 * expert_count))
    slot_total = expert_count * capacity

    half_width = model_width // 2
    pieces = []
    rest = gate_probs
    for _ in range(3):
        piece = lax.reduce_precision(rest, exponent_bits=8, mantissa_bits=7)
        pieces.append(piece)
        rest = rest - piece
    meta = jnp.concatenate([expert_ids.astype(jnp.float32)] + pieces, axis=1)
    meta_width = 128
    meta = jnp.pad(meta, ((0, 0), (0, meta_width - meta.shape[1]))).astype(jnp.bfloat16)
    first = lax.all_gather(
        jnp.concatenate([tokens, cotangent[:, :half_width], meta], axis=1), "expert", axis=0
    )
    first, cot_after = lax.optimization_barrier((first, cotangent))
    cot_hi = lax.all_gather(cot_after[:, half_width:], "expert", axis=0)
    meta_at = model_width + half_width
    all_meta = first[..., meta_at : meta_at + 4 * top_count].astype(jnp.float32)
    all_ids = all_meta[..., :top_count].astype(jnp.int32)
    all_gates = (
        all_meta[..., top_count : 2 * top_count] + all_meta[..., 2 * top_count : 3 * top_count]
    ) + all_meta[..., 3 * top_count :]


    match = all_ids == me
    routed = jnp.any(match, axis=-1).astype(jnp.float32)
    gate_of = jnp.sum(jnp.where(match, all_gates, 0.0), axis=-1)
    rank = exclusive_count(routed)
    slots = jnp.arange(capacity, dtype=jnp.float32)
    pick = (routed[:, None, :] > 0) & (rank[:, None, :] == slots[None, :, None])
    pick_b = pick.astype(jnp.bfloat16)
    picked_first = jnp.einsum(
        "srt,stc->src", pick_b, first, preferred_element_type=jnp.float32
    ).astype(jnp.bfloat16)
    inputs = picked_first[..., :model_width]
    slot_gate = jnp.sum(jnp.where(pick, gate_of[:, None, :], 0.0), axis=-1)
    picked_hi = jnp.einsum(
        "srt,stc->src", pick_b, cot_hi, preferred_element_type=jnp.float32
    ).astype(jnp.bfloat16)
    scaled = [
        (slot_gate[..., None] * part.astype(jnp.float32))
        .astype(jnp.bfloat16)
        .reshape(slot_total, half_width)
        for part in (picked_first[..., model_width:meta_at], picked_hi)
    ]

    weight_pair = gate_up[0]
    weight_down = down_weight[0]
    grad_pair, grad_down, row_grads = expert_backward(
        inputs.reshape(slot_total, model_width),
        scaled,
        weight_pair,
        weight_down,
    )
    dense = jnp.einsum(
        "srt,src->stc",
        pick_b,
        row_grads.reshape(expert_count, capacity, model_width),
        preferred_element_type=jnp.float32,
    ).astype(jnp.bfloat16)
    token_grad = lax.psum_scatter(
        dense.reshape(expert_count * local_tokens, model_width),
        "expert",
        scatter_dimension=0,
        tiled=True,
    )

    groups = lax.axis_size("group")
    share_rows = model_width // groups
    hidden_count = grad_down.shape[0]
    pair_width = grad_pair.shape[1]
    pair_parts = lax.all_to_all(
        grad_pair.astype(jnp.bfloat16).reshape(groups, share_rows, pair_width),
        "group", 0, 0, tiled=True,
    )
    down_parts = lax.all_to_all(
        grad_down.astype(jnp.bfloat16).reshape(hidden_count, groups, share_rows),
        "group", 1, 1, tiled=True,
    )
    sum_pair = jnp.sum(pair_parts.astype(jnp.float32), axis=0)[None]
    sum_down = jnp.sum(down_parts.astype(jnp.float32), axis=1)[None]
    group_index = lax.axis_index("group")
    own_pair = lax.dynamic_slice_in_dim(gate_up, group_index * share_rows, share_rows, 1)
    own_down = lax.dynamic_slice_in_dim(down_weight, group_index * share_rows, share_rows, 2)
    new_pair, first_pair, second_pair = adam_update(
        own_pair, sum_pair, gate_up_moment, gate_up_second
    )
    new_down, first_down, second_down = adam_update(own_down, sum_down, down_moment, down_second)
    full_pair = lax.all_to_all(
        jnp.broadcast_to(new_pair, (groups, share_rows, pair_width)), "group", 0, 0, tiled=True
    ).reshape(1, model_width, pair_width)
    full_down = lax.all_to_all(
        jnp.broadcast_to(new_down.reshape(hidden_count, 1, share_rows), (hidden_count, groups, share_rows)),
        "group", 1, 1, tiled=True,
    ).reshape(1, hidden_count, model_width)
    return (token_grad, full_pair, full_down, first_pair, second_pair, first_down, second_down)


def solution(mesh):
    rows = P(("group", "expert"), None)
    placed = (
        rows,
        rows,
        rows,
        rows,
        P("expert", None, None),
        P("expert", None, None),
        P("expert", "group", None),
        P("expert", "group", None),
        P("expert", None, "group"),
        P("expert", None, "group"),
    )
    return jax.shard_map(
        local,
        mesh=mesh,
        in_specs=placed,
        out_specs=(
            rows,
            P("expert", None, None),
            P("expert", None, None),
            P("expert", "group", None),
            P("expert", "group", None),
            P("expert", None, "group"),
            P("expert", None, "group"),
        ),
        check_vma=False,
    )
```

```python
import jax
import jax.numpy as jnp
from jax import lax
from jax.sharding import PartitionSpec as P

learn_rate = 0.001
beta_first = 0.9
beta_second = 0.999
adam_eps = 1e-08


def expert_backward(inputs, scaled_parts, weight_gate_up, weight_down):
    hidden_count = weight_down.shape[0]
    width = scaled_parts[0].shape[1]
    projected = jnp.dot(inputs, weight_gate_up, preferred_element_type=jnp.float32)
    gate_part = projected[:, :hidden_count]
    up_part = projected[:, hidden_count:]
    sigmoid_gate = jax.nn.sigmoid(gate_part)
    activated = gate_part * sigmoid_gate
    hidden_act = (activated * up_part).astype(jnp.bfloat16)
    hidden_grad = sum(
        jnp.dot(part, weight_down[:, i * width : (i + 1) * width].T, preferred_element_type=jnp.float32)
        for i, part in enumerate(scaled_parts)
    )
    slope = sigmoid_gate * (1.0 + gate_part * (1.0 - sigmoid_gate))
    hidden_act, up_slope, activated = lax.optimization_barrier(
        (hidden_act, up_part * slope, activated)
    )
    pair_grad = jnp.concatenate(
        [hidden_grad * up_slope, hidden_grad * activated], axis=1
    ).astype(jnp.bfloat16)
    down_grad = jnp.concatenate(
        [jnp.dot(hidden_act.T, part, preferred_element_type=jnp.float32) for part in scaled_parts],
        axis=1,
    )
    gate_up_grad = jnp.dot(inputs.T, pair_grad, preferred_element_type=jnp.float32)
    input_grad = jnp.dot(pair_grad, weight_gate_up.T, preferred_element_type=jnp.float32).astype(
        jnp.bfloat16
    )
    return (gate_up_grad, down_grad, input_grad)


def adam_update(weight, grad, first, second):
    first_new = beta_first * first + (1.0 - beta_first) * grad
    second_new = beta_second * second + (1.0 - beta_second) * grad * grad
    updated = (
        weight.astype(jnp.float32) - learn_rate * first_new / (jnp.sqrt(second_new) + adam_eps)
    ).astype(jnp.bfloat16)
    return (updated, first_new, second_new)


def exclusive_count(flags):
    n = flags.shape[-1]
    earlier = (jnp.arange(n)[:, None] < jnp.arange(n)[None, :]).astype(jnp.bfloat16)
    return jnp.dot(flags.astype(jnp.bfloat16), earlier, preferred_element_type=jnp.float32)


def local(
    tokens,
    cotangent,
    gate_probs,
    expert_ids,
    gate_up,
    down_weight,
    gate_up_moment,
    gate_up_second,
    down_moment,
    down_second,
):
    expert_count = lax.axis_size("expert")
    me = lax.axis_index("expert")
    local_tokens, model_width = tokens.shape
    top_count = expert_ids.shape[1]
    capacity = min(local_tokens, 9 * local_tokens * top_count // (4 * expert_count))
    slot_total = expert_count * capacity

    half_width = model_width // 2
    pieces = []
    rest = gate_probs
    for _ in range(3):
        piece = lax.reduce_precision(rest, exponent_bits=8, mantissa_bits=7)
        pieces.append(piece)
        rest = rest - piece
    meta = jnp.concatenate([expert_ids.astype(jnp.float32)] + pieces, axis=1)
    meta_width = 128
    meta = jnp.pad(meta, ((0, 0), (0, meta_width - meta.shape[1]))).astype(jnp.bfloat16)
    first = lax.all_gather(
        jnp.concatenate([tokens, cotangent[:, :half_width], meta], axis=1), "expert", axis=0
    )
    first, cot_after = lax.optimization_barrier((first, cotangent))
    cot_hi = lax.all_gather(cot_after[:, half_width:], "expert", axis=0)
    meta_at = model_width + half_width
    all_meta = first[..., meta_at : meta_at + 4 * top_count].astype(jnp.float32)
    all_ids = all_meta[..., :top_count].astype(jnp.int32)
    all_gates = (
        all_meta[..., top_count : 2 * top_count] + all_meta[..., 2 * top_count : 3 * top_count]
    ) + all_meta[..., 3 * top_count :]


    match = all_ids == me
    routed = jnp.any(match, axis=-1).astype(jnp.float32)
    gate_of = jnp.sum(jnp.where(match, all_gates, 0.0), axis=-1)
    rank = exclusive_count(routed)
    slots = jnp.arange(capacity, dtype=jnp.float32)
    pick = (routed[:, None, :] > 0) & (rank[:, None, :] == slots[None, :, None])
    pick_b = pick.astype(jnp.bfloat16)
    picked_first = jnp.einsum(
        "srt,stc->src", pick_b, first, preferred_element_type=jnp.float32
    ).astype(jnp.bfloat16)
    inputs = picked_first[..., :model_width]
    slot_gate = jnp.sum(jnp.where(pick, gate_of[:, None, :], 0.0), axis=-1)
    picked_hi = jnp.einsum(
        "srt,stc->src", pick_b, cot_hi, preferred_element_type=jnp.float32
    ).astype(jnp.bfloat16)
    scaled = [
        (slot_gate[..., None] * part.astype(jnp.float32))
        .astype(jnp.bfloat16)
        .reshape(slot_total, half_width)
        for part in (picked_first[..., model_width:meta_at], picked_hi)
    ]

    weight_pair = gate_up[0]
    weight_down = down_weight[0]
    grad_pair, grad_down, row_grads = expert_backward(
        inputs.reshape(slot_total, model_width),
        scaled,
        weight_pair,
        weight_down,
    )
    dense = jnp.einsum(
        "srt,src->stc",
        pick_b,
        row_grads.reshape(expert_count, capacity, model_width),
        preferred_element_type=jnp.float32,
    ).astype(jnp.bfloat16)
    token_grad = lax.psum_scatter(
        dense.reshape(expert_count * local_tokens, model_width),
        "expert",
        scatter_dimension=0,
        tiled=True,
    )

    groups = lax.axis_size("group")
    share_rows = model_width // groups
    hidden_count = grad_down.shape[0]
    pair_width = grad_pair.shape[1]
    pair_parts = lax.all_to_all(
        grad_pair.astype(jnp.bfloat16).reshape(groups, share_rows, pair_width),
        "group", 0, 0, tiled=True,
    )
    down_parts = lax.all_to_all(
        grad_down.astype(jnp.bfloat16).reshape(hidden_count, groups, share_rows),
        "group", 1, 1, tiled=True,
    )
    sum_pair = jnp.sum(pair_parts.astype(jnp.float32), axis=0)[None]
    sum_down = jnp.sum(down_parts.astype(jnp.float32), axis=1)[None]
    group_index = lax.axis_index("group")
    own_pair = lax.dynamic_slice_in_dim(gate_up, group_index * share_rows, share_rows, 1)
    own_down = lax.dynamic_slice_in_dim(down_weight, group_index * share_rows, share_rows, 2)
    new_pair, first_pair, second_pair = adam_update(
        own_pair, sum_pair, gate_up_moment, gate_up_second
    )
    new_down, first_down, second_down = adam_update(own_down, sum_down, down_moment, down_second)
    full_pair = lax.all_to_all(
        jnp.broadcast_to(new_pair, (groups, share_rows, pair_width)), "group", 0, 0, tiled=True
    ).reshape(1, model_width, pair_width)
    full_down = lax.all_gather(new_down, "group", axis=2, tiled=True)
    return (token_grad, full_pair, full_down, first_pair, second_pair, first_down, second_down)


def solution(mesh):
    rows = P(("group", "expert"), None)
    placed = (
        rows,
        rows,
        rows,
        rows,
        P("expert", None, None),
        P("expert", None, None),
        P("expert", "group", None),
        P("expert", "group", None),
        P("expert", None, "group"),
        P("expert", None, "group"),
    )
    return jax.shard_map(
        local,
        mesh=mesh,
        in_specs=placed,
        out_specs=(
            rows,
            P("expert", None, None),
            P("expert", None, None),
            P("expert", "group", None),
            P("expert", "group", None),
            P("expert", None, "group"),
            P("expert", None, "group"),
        ),
        check_vma=False,
    )
```

```python
import jax
import jax.numpy as jnp
from jax import lax
from jax.sharding import PartitionSpec as P

learn_rate = 0.001
beta_first = 0.9
beta_second = 0.999
adam_eps = 1e-08


def expert_backward(inputs, scaled_parts, weight_gate_up, weight_down):
    hidden_count = weight_down.shape[0]
    width = scaled_parts[0].shape[1]
    projected = jnp.dot(inputs, weight_gate_up, preferred_element_type=jnp.float32)
    gate_part = projected[:, :hidden_count]
    up_part = projected[:, hidden_count:]
    sigmoid_gate = jax.nn.sigmoid(gate_part)
    activated = gate_part * sigmoid_gate
    hidden_act = (activated * up_part).astype(jnp.bfloat16)
    hidden_grad = sum(
        jnp.dot(part, weight_down[:, i * width : (i + 1) * width].T, preferred_element_type=jnp.float32)
        for i, part in enumerate(scaled_parts)
    )
    slope = sigmoid_gate * (1.0 + gate_part * (1.0 - sigmoid_gate))
    hidden_act, up_slope, activated = lax.optimization_barrier(
        (hidden_act, up_part * slope, activated)
    )
    pair_grad = jnp.concatenate(
        [hidden_grad * up_slope, hidden_grad * activated], axis=1
    ).astype(jnp.bfloat16)
    down_grad = jnp.concatenate(
        [jnp.dot(hidden_act.T, part, preferred_element_type=jnp.float32) for part in scaled_parts],
        axis=1,
    )
    gate_up_grad = jnp.dot(inputs.T, pair_grad, preferred_element_type=jnp.float32)
    input_grad = jnp.dot(pair_grad, weight_gate_up.T, preferred_element_type=jnp.float32).astype(
        jnp.bfloat16
    )
    return (gate_up_grad, down_grad, input_grad)


def adam_update(weight, grad, first, second):
    first_new = beta_first * first + (1.0 - beta_first) * grad
    second_new = beta_second * second + (1.0 - beta_second) * grad * grad
    updated = (
        weight.astype(jnp.float32) - learn_rate * first_new / (jnp.sqrt(second_new) + adam_eps)
    ).astype(jnp.bfloat16)
    return (updated, first_new, second_new)


def exclusive_count(flags):
    n = flags.shape[-1]
    earlier = (jnp.arange(n)[:, None] < jnp.arange(n)[None, :]).astype(jnp.bfloat16)
    return jnp.dot(flags.astype(jnp.bfloat16), earlier, preferred_element_type=jnp.float32)


def local(
    tokens,
    cotangent,
    gate_probs,
    expert_ids,
    gate_up,
    down_weight,
    gate_up_moment,
    gate_up_second,
    down_moment,
    down_second,
):
    expert_count = lax.axis_size("expert")
    me = lax.axis_index("expert")
    local_tokens, model_width = tokens.shape
    top_count = expert_ids.shape[1]
    capacity = min(local_tokens, 9 * local_tokens * top_count // (4 * expert_count))
    slot_total = expert_count * capacity

    half_width = model_width // 2
    pieces = []
    rest = gate_probs
    for _ in range(3):
        piece = lax.reduce_precision(rest, exponent_bits=8, mantissa_bits=7)
        pieces.append(piece)
        rest = rest - piece
    meta = jnp.concatenate([expert_ids.astype(jnp.float32)] + pieces, axis=1)
    meta_width = 128
    meta = jnp.pad(meta, ((0, 0), (0, meta_width - meta.shape[1]))).astype(jnp.bfloat16)
    first = lax.all_gather(
        jnp.concatenate([tokens, cotangent[:, :half_width], meta], axis=1), "expert", axis=0
    )
    first, cot_after = lax.optimization_barrier((first, cotangent))
    cot_hi = lax.all_gather(cot_after[:, half_width:], "expert", axis=0)
    meta_at = model_width + half_width
    all_meta = first[..., meta_at : meta_at + 4 * top_count].astype(jnp.float32)
    all_ids = all_meta[..., :top_count].astype(jnp.int32)
    all_gates = (
        all_meta[..., top_count : 2 * top_count] + all_meta[..., 2 * top_count : 3 * top_count]
    ) + all_meta[..., 3 * top_count :]


    match = all_ids == me
    routed = jnp.any(match, axis=-1).astype(jnp.float32)
    gate_of = jnp.sum(jnp.where(match, all_gates, 0.0), axis=-1)
    rank = exclusive_count(routed)
    slots = jnp.arange(capacity, dtype=jnp.float32)
    pick = (routed[:, None, :] > 0) & (rank[:, None, :] == slots[None, :, None])
    pick_b = pick.astype(jnp.bfloat16)
    picked_first = jnp.einsum(
        "srt,stc->src", pick_b, first, preferred_element_type=jnp.float32
    ).astype(jnp.bfloat16)
    inputs = picked_first[..., :model_width]
    slot_gate = jnp.sum(jnp.where(pick, gate_of[:, None, :], 0.0), axis=-1)
    picked_hi = jnp.einsum(
        "srt,stc->src", pick_b, cot_hi, preferred_element_type=jnp.float32
    ).astype(jnp.bfloat16)
    scaled = [
        (slot_gate[..., None] * part.astype(jnp.float32))
        .astype(jnp.bfloat16)
        .reshape(slot_total, half_width)
        for part in (picked_first[..., model_width:meta_at], picked_hi)
    ]

    weight_pair = gate_up[0]
    weight_down = down_weight[0]
    grad_pair, grad_down, row_grads = expert_backward(
        inputs.reshape(slot_total, model_width),
        scaled,
        weight_pair,
        weight_down,
    )
    dense = jnp.einsum(
        "srt,src->stc",
        pick_b,
        row_grads.reshape(expert_count, capacity, model_width),
        preferred_element_type=jnp.float32,
    ).astype(jnp.bfloat16)
    token_grad = lax.psum_scatter(
        dense.reshape(expert_count * local_tokens, model_width),
        "expert",
        scatter_dimension=0,
        tiled=True,
    )

    groups = lax.axis_size("group")
    share_rows = model_width // groups
    hidden_count = grad_down.shape[0]
    pair_width = grad_pair.shape[1]
    pair_parts = lax.all_to_all(
        grad_pair.astype(jnp.bfloat16).reshape(groups, share_rows, pair_width),
        "group", 0, 0, tiled=True,
    )
    down_parts = lax.all_to_all(
        grad_down.astype(jnp.bfloat16).reshape(hidden_count, groups, share_rows),
        "group", 1, 1, tiled=True,
    )
    sum_pair = jnp.sum(pair_parts.astype(jnp.float32), axis=0)[None]
    sum_down = jnp.sum(down_parts.astype(jnp.float32), axis=1)[None]
    token_grad, sum_down = lax.optimization_barrier((token_grad, sum_down))
    group_index = lax.axis_index("group")
    own_pair = lax.dynamic_slice_in_dim(gate_up, group_index * share_rows, share_rows, 1)
    own_down = lax.dynamic_slice_in_dim(down_weight, group_index * share_rows, share_rows, 2)
    new_pair, first_pair, second_pair = adam_update(
        own_pair, sum_pair, gate_up_moment, gate_up_second
    )
    new_down, first_down, second_down = adam_update(own_down, sum_down, down_moment, down_second)
    full_pair = lax.all_to_all(
        jnp.broadcast_to(new_pair, (groups, share_rows, pair_width)), "group", 0, 0, tiled=True
    ).reshape(1, model_width, pair_width)
    full_down = lax.all_gather(new_down, "group", axis=2, tiled=True)
    return (token_grad, full_pair, full_down, first_pair, second_pair, first_down, second_down)


def solution(mesh):
    rows = P(("group", "expert"), None)
    placed = (
        rows,
        rows,
        rows,
        rows,
        P("expert", None, None),
        P("expert", None, None),
        P("expert", "group", None),
        P("expert", "group", None),
        P("expert", None, "group"),
        P("expert", None, "group"),
    )
    return jax.shard_map(
        local,
        mesh=mesh,
        in_specs=placed,
        out_specs=(
            rows,
            P("expert", None, None),
            P("expert", None, None),
            P("expert", "group", None),
            P("expert", "group", None),
            P("expert", None, "group"),
            P("expert", None, "group"),
        ),
        check_vma=False,
    )
```

```python
import jax
import jax.numpy as jnp
from jax import lax
from jax.sharding import PartitionSpec as P

learn_rate = 0.001
beta_first = 0.9
beta_second = 0.999
adam_eps = 1e-08


def expert_backward(inputs, scaled_parts, weight_gate_up, weight_down):
    hidden_count = weight_down.shape[0]
    width = scaled_parts[0].shape[1]
    projected = jnp.dot(inputs, weight_gate_up, preferred_element_type=jnp.float32)
    gate_part = projected[:, :hidden_count]
    up_part = projected[:, hidden_count:]
    sigmoid_gate = jax.nn.sigmoid(gate_part)
    activated = gate_part * sigmoid_gate
    hidden_act = (activated * up_part).astype(jnp.bfloat16)
    hidden_grad = sum(
        jnp.dot(part, weight_down[:, i * width : (i + 1) * width].T, preferred_element_type=jnp.float32)
        for i, part in enumerate(scaled_parts)
    )
    slope = sigmoid_gate * (1.0 + gate_part * (1.0 - sigmoid_gate))
    hidden_act, up_slope, activated = lax.optimization_barrier(
        (hidden_act, up_part * slope, activated)
    )
    pair_grad = jnp.concatenate(
        [hidden_grad * up_slope, hidden_grad * activated], axis=1
    ).astype(jnp.bfloat16)
    down_grad = jnp.dot(
        hidden_act.T, jnp.concatenate(scaled_parts, axis=1), preferred_element_type=jnp.float32
    )
    gate_up_grad = jnp.dot(inputs.T, pair_grad, preferred_element_type=jnp.float32)
    input_grad = jnp.dot(pair_grad, weight_gate_up.T, preferred_element_type=jnp.float32).astype(
        jnp.bfloat16
    )
    return (gate_up_grad, down_grad, input_grad)


def adam_update(weight, grad, first, second):
    first_new = beta_first * first + (1.0 - beta_first) * grad
    second_new = beta_second * second + (1.0 - beta_second) * grad * grad
    updated = (
        weight.astype(jnp.float32) - learn_rate * first_new / (jnp.sqrt(second_new) + adam_eps)
    ).astype(jnp.bfloat16)
    return (updated, first_new, second_new)


def exclusive_count(flags):
    n = flags.shape[-1]
    earlier = (jnp.arange(n)[:, None] < jnp.arange(n)[None, :]).astype(jnp.bfloat16)
    return jnp.dot(flags.astype(jnp.bfloat16), earlier, preferred_element_type=jnp.float32)


def local(
    tokens,
    cotangent,
    gate_probs,
    expert_ids,
    gate_up,
    down_weight,
    gate_up_moment,
    gate_up_second,
    down_moment,
    down_second,
):
    expert_count = lax.axis_size("expert")
    me = lax.axis_index("expert")
    local_tokens, model_width = tokens.shape
    top_count = expert_ids.shape[1]
    capacity = min(local_tokens, 9 * local_tokens * top_count // (4 * expert_count))
    slot_total = expert_count * capacity

    half_width = model_width // 2
    pieces = []
    rest = gate_probs
    for _ in range(3):
        piece = lax.reduce_precision(rest, exponent_bits=8, mantissa_bits=7)
        pieces.append(piece)
        rest = rest - piece
    meta = jnp.concatenate([expert_ids.astype(jnp.float32)] + pieces, axis=1)
    meta_width = 128
    meta = jnp.pad(meta, ((0, 0), (0, meta_width - meta.shape[1]))).astype(jnp.bfloat16)
    first = lax.all_gather(
        jnp.concatenate([tokens, cotangent[:, :half_width], meta], axis=1), "expert", axis=0
    )
    first, cot_after = lax.optimization_barrier((first, cotangent))
    cot_hi = lax.all_gather(cot_after[:, half_width:], "expert", axis=0)
    meta_at = model_width + half_width
    all_meta = first[..., meta_at : meta_at + 4 * top_count].astype(jnp.float32)
    all_ids = all_meta[..., :top_count].astype(jnp.int32)
    all_gates = (
        all_meta[..., top_count : 2 * top_count] + all_meta[..., 2 * top_count : 3 * top_count]
    ) + all_meta[..., 3 * top_count :]


    match = all_ids == me
    routed = jnp.any(match, axis=-1).astype(jnp.float32)
    gate_of = jnp.sum(jnp.where(match, all_gates, 0.0), axis=-1)
    rank = exclusive_count(routed)
    slots = jnp.arange(capacity, dtype=jnp.float32)
    pick = (routed[:, None, :] > 0) & (rank[:, None, :] == slots[None, :, None])
    pick_b = pick.astype(jnp.bfloat16)
    picked_first = jnp.einsum(
        "srt,stc->src", pick_b, first, preferred_element_type=jnp.float32
    ).astype(jnp.bfloat16)
    inputs = picked_first[..., :model_width]
    slot_gate = jnp.sum(jnp.where(pick, gate_of[:, None, :], 0.0), axis=-1)
    picked_hi = jnp.einsum(
        "srt,stc->src", pick_b, cot_hi, preferred_element_type=jnp.float32
    ).astype(jnp.bfloat16)
    scaled = [
        (slot_gate[..., None] * part.astype(jnp.float32))
        .astype(jnp.bfloat16)
        .reshape(slot_total, half_width)
        for part in (picked_first[..., model_width:meta_at], picked_hi)
    ]

    weight_pair = gate_up[0]
    weight_down = down_weight[0]
    grad_pair, grad_down, row_grads = expert_backward(
        inputs.reshape(slot_total, model_width),
        scaled,
        weight_pair,
        weight_down,
    )
    dense = jnp.einsum(
        "srt,src->stc",
        pick_b,
        row_grads.reshape(expert_count, capacity, model_width),
        preferred_element_type=jnp.float32,
    ).astype(jnp.bfloat16)
    token_grad = lax.psum_scatter(
        dense.reshape(expert_count * local_tokens, model_width),
        "expert",
        scatter_dimension=0,
        tiled=True,
    )

    groups = lax.axis_size("group")
    share_rows = model_width // groups
    hidden_count = grad_down.shape[0]
    pair_width = grad_pair.shape[1]
    pair_parts = lax.all_to_all(
        grad_pair.astype(jnp.bfloat16).reshape(groups, share_rows, pair_width),
        "group", 0, 0, tiled=True,
    )
    down_parts = lax.all_to_all(
        grad_down.astype(jnp.bfloat16).reshape(hidden_count, groups, share_rows),
        "group", 1, 1, tiled=True,
    )
    sum_pair = jnp.sum(pair_parts.astype(jnp.float32), axis=0)[None]
    sum_down = jnp.sum(down_parts.astype(jnp.float32), axis=1)[None]
    token_grad, sum_down = lax.optimization_barrier((token_grad, sum_down))
    group_index = lax.axis_index("group")
    own_pair = lax.dynamic_slice_in_dim(gate_up, group_index * share_rows, share_rows, 1)
    own_down = lax.dynamic_slice_in_dim(down_weight, group_index * share_rows, share_rows, 2)
    new_pair, first_pair, second_pair = adam_update(
        own_pair, sum_pair, gate_up_moment, gate_up_second
    )
    new_down, first_down, second_down = adam_update(own_down, sum_down, down_moment, down_second)
    full_pair = lax.all_to_all(
        jnp.broadcast_to(new_pair, (groups, share_rows, pair_width)), "group", 0, 0, tiled=True
    ).reshape(1, model_width, pair_width)
    full_down = lax.all_gather(new_down, "group", axis=2, tiled=True)
    return (token_grad, full_pair, full_down, first_pair, second_pair, first_down, second_down)


def solution(mesh):
    rows = P(("group", "expert"), None)
    placed = (
        rows,
        rows,
        rows,
        rows,
        P("expert", None, None),
        P("expert", None, None),
        P("expert", "group", None),
        P("expert", "group", None),
        P("expert", None, "group"),
        P("expert", None, "group"),
    )
    return jax.shard_map(
        local,
        mesh=mesh,
        in_specs=placed,
        out_specs=(
            rows,
            P("expert", None, None),
            P("expert", None, None),
            P("expert", "group", None),
            P("expert", "group", None),
            P("expert", None, "group"),
            P("expert", None, "group"),
        ),
        check_vma=False,
    )
```

```python
import jax
import jax.numpy as jnp
from jax import lax
from jax.sharding import PartitionSpec as P

learn_rate = 0.001
beta_first = 0.9
beta_second = 0.999
adam_eps = 1e-08


def expert_backward(inputs, scaled_parts, weight_gate_up, weight_down):
    hidden_count = weight_down.shape[0]
    width = scaled_parts[0].shape[1]
    projected = jnp.dot(inputs, weight_gate_up, preferred_element_type=jnp.float32)
    gate_part = projected[:, :hidden_count]
    up_part = projected[:, hidden_count:]
    sigmoid_gate = jax.nn.sigmoid(gate_part)
    activated = gate_part * sigmoid_gate
    hidden_act = (activated * up_part).astype(jnp.bfloat16)
    hidden_grad = sum(
        jnp.dot(part, weight_down[:, i * width : (i + 1) * width].T, preferred_element_type=jnp.float32)
        for i, part in enumerate(scaled_parts)
    )
    slope = sigmoid_gate * (1.0 + gate_part * (1.0 - sigmoid_gate))
    hidden_act, up_slope, activated = lax.optimization_barrier(
        (hidden_act, up_part * slope, activated)
    )
    pair_grad = jnp.concatenate(
        [hidden_grad * up_slope, hidden_grad * activated], axis=1
    ).astype(jnp.bfloat16)
    down_grad = jnp.dot(
        hidden_act.T, jnp.concatenate(scaled_parts, axis=1), preferred_element_type=jnp.float32
    )
    gate_up_grad = jnp.dot(inputs.T, pair_grad, preferred_element_type=jnp.float32)
    input_grad = jnp.dot(pair_grad, weight_gate_up.T, preferred_element_type=jnp.float32).astype(
        jnp.bfloat16
    )
    return (gate_up_grad, down_grad, input_grad)


def adam_update(weight, grad, first, second):
    first_new = beta_first * first + (1.0 - beta_first) * grad
    second_new = beta_second * second + (1.0 - beta_second) * grad * grad
    updated = (
        weight.astype(jnp.float32) - learn_rate * first_new / (jnp.sqrt(second_new) + adam_eps)
    ).astype(jnp.bfloat16)
    return (updated, first_new, second_new)


def exclusive_count(flags):
    n = flags.shape[-1]
    earlier = (jnp.arange(n)[:, None] < jnp.arange(n)[None, :]).astype(jnp.bfloat16)
    return jnp.dot(flags.astype(jnp.bfloat16), earlier, preferred_element_type=jnp.float32)


def local(
    tokens,
    cotangent,
    gate_probs,
    expert_ids,
    gate_up,
    down_weight,
    gate_up_moment,
    gate_up_second,
    down_moment,
    down_second,
):
    expert_count = lax.axis_size("expert")
    me = lax.axis_index("expert")
    local_tokens, model_width = tokens.shape
    top_count = expert_ids.shape[1]
    capacity = min(local_tokens, 9 * local_tokens * top_count // (4 * expert_count))
    slot_total = expert_count * capacity

    half_width = model_width // 2
    pieces = []
    rest = gate_probs
    for _ in range(3):
        piece = lax.reduce_precision(rest, exponent_bits=8, mantissa_bits=7)
        pieces.append(piece)
        rest = rest - piece
    meta = jnp.concatenate([expert_ids.astype(jnp.float32)] + pieces, axis=1)
    meta_width = 128
    meta = jnp.pad(meta, ((0, 0), (0, meta_width - meta.shape[1]))).astype(jnp.bfloat16)
    first = lax.all_gather(
        jnp.concatenate([tokens, cotangent[:, :half_width], meta], axis=1), "expert", axis=0
    )
    first, cot_after = lax.optimization_barrier((first, cotangent))
    cot_hi = lax.all_gather(cot_after[:, half_width:], "expert", axis=0)
    meta_at = model_width + half_width
    all_meta = first[..., meta_at : meta_at + 4 * top_count].astype(jnp.float32)
    all_ids = all_meta[..., :top_count].astype(jnp.int32)
    all_gates = (
        all_meta[..., top_count : 2 * top_count] + all_meta[..., 2 * top_count : 3 * top_count]
    ) + all_meta[..., 3 * top_count :]


    match = all_ids == me
    routed = jnp.any(match, axis=-1).astype(jnp.float32)
    gate_of = jnp.sum(jnp.where(match, all_gates, 0.0), axis=-1)
    rank = exclusive_count(routed)
    slots = jnp.arange(capacity, dtype=jnp.float32)
    pick = (routed[:, None, :] > 0) & (rank[:, None, :] == slots[None, :, None])
    pick_b = pick.astype(jnp.bfloat16)
    picked_first = jnp.einsum(
        "srt,stc->src", pick_b, first, preferred_element_type=jnp.float32
    ).astype(jnp.bfloat16)
    inputs = picked_first[..., :model_width]
    slot_gate = jnp.sum(jnp.where(pick, gate_of[:, None, :], 0.0), axis=-1)
    picked_hi = jnp.einsum(
        "srt,stc->src", pick_b, cot_hi, preferred_element_type=jnp.float32
    ).astype(jnp.bfloat16)
    scaled = [
        (slot_gate[..., None] * part.astype(jnp.float32))
        .astype(jnp.bfloat16)
        .reshape(slot_total, half_width)
        for part in (picked_first[..., model_width:meta_at], picked_hi)
    ]

    weight_pair = gate_up[0]
    weight_down = down_weight[0]
    grad_pair, grad_down, row_grads = expert_backward(
        inputs.reshape(slot_total, model_width),
        scaled,
        weight_pair,
        weight_down,
    )
    dense = jnp.einsum(
        "srt,src->stc",
        pick_b,
        row_grads.reshape(expert_count, capacity, model_width),
        preferred_element_type=jnp.float32,
    ).astype(jnp.bfloat16)
    token_grad = lax.psum_scatter(
        dense.reshape(expert_count * local_tokens, model_width),
        "expert",
        scatter_dimension=0,
        tiled=True,
    )

    groups = lax.axis_size("group")
    share_rows = model_width // groups
    hidden_count = grad_down.shape[0]
    pair_width = grad_pair.shape[1]
    pair_parts = lax.all_to_all(
        grad_pair.astype(jnp.bfloat16).reshape(groups, share_rows, pair_width),
        "group", 0, 0, tiled=True,
    )
    down_parts = lax.all_to_all(
        grad_down.astype(jnp.bfloat16).reshape(hidden_count, groups, share_rows),
        "group", 1, 1, tiled=True,
    )
    sum_pair = jnp.sum(pair_parts.astype(jnp.float32), axis=0)[None]
    sum_down = jnp.sum(down_parts.astype(jnp.float32), axis=1)[None]
    token_grad, sum_down = lax.optimization_barrier((token_grad, sum_down))
    group_index = lax.axis_index("group")
    own_pair = lax.dynamic_slice_in_dim(gate_up, group_index * share_rows, share_rows, 1)
    own_down = lax.dynamic_slice_in_dim(down_weight, group_index * share_rows, share_rows, 2)
    new_pair, first_pair, second_pair = adam_update(
        own_pair, sum_pair, gate_up_moment, gate_up_second
    )
    new_down, first_down, second_down = adam_update(own_down, sum_down, down_moment, down_second)
    full_pair = lax.all_to_all(
        jnp.broadcast_to(new_pair, (groups, share_rows, pair_width)), "group", 0, 0, tiled=True
    ).reshape(1, model_width, pair_width)
    by_shift = [new_down[0]]
    for shift in range(1, groups):
        pairs = [(i, (i + shift) % groups) for i in range(groups)]
        by_shift.append(lax.ppermute(new_down[0], "group", pairs))
    ahead = jnp.stack([by_shift[(-k) % groups] for k in range(groups)])
    by_member = jnp.roll(ahead, group_index, axis=0)
    full_down = by_member.transpose(1, 0, 2).reshape(1, hidden_count, model_width)
    return (token_grad, full_pair, full_down, first_pair, second_pair, first_down, second_down)


def solution(mesh):
    rows = P(("group", "expert"), None)
    placed = (
        rows,
        rows,
        rows,
        rows,
        P("expert", None, None),
        P("expert", None, None),
        P("expert", "group", None),
        P("expert", "group", None),
        P("expert", None, "group"),
        P("expert", None, "group"),
    )
    return jax.shard_map(
        local,
        mesh=mesh,
        in_specs=placed,
        out_specs=(
            rows,
            P("expert", None, None),
            P("expert", None, None),
            P("expert", "group", None),
            P("expert", "group", None),
            P("expert", None, "group"),
            P("expert", None, "group"),
        ),
        check_vma=False,
    )
```

```python
import jax
import jax.numpy as jnp
from jax import lax
from jax.sharding import PartitionSpec as P

learn_rate = 0.001
beta_first = 0.9
beta_second = 0.999
adam_eps = 1e-08


def expert_backward(inputs, scaled_parts, weight_gate_up, weight_down):
    hidden_count = weight_down.shape[0]
    width = scaled_parts[0].shape[1]
    projected = jnp.dot(inputs, weight_gate_up, preferred_element_type=jnp.float32)
    gate_part = projected[:, :hidden_count]
    up_part = projected[:, hidden_count:]
    sigmoid_gate = jax.nn.sigmoid(gate_part)
    activated = gate_part * sigmoid_gate
    hidden_act = (activated * up_part).astype(jnp.bfloat16)
    hidden_grad = sum(
        jnp.dot(part, weight_down[:, i * width : (i + 1) * width].T, preferred_element_type=jnp.float32)
        for i, part in enumerate(scaled_parts)
    )
    slope = sigmoid_gate * (1.0 + gate_part * (1.0 - sigmoid_gate))
    up_slope = up_part * slope
    pair_grad = jnp.concatenate(
        [hidden_grad * up_slope, hidden_grad * activated], axis=1
    ).astype(jnp.bfloat16)
    down_grad = jnp.dot(
        hidden_act.T, jnp.concatenate(scaled_parts, axis=1), preferred_element_type=jnp.float32
    )
    gate_up_grad = jnp.dot(inputs.T, pair_grad, preferred_element_type=jnp.float32)
    input_grad = jnp.dot(pair_grad, weight_gate_up.T, preferred_element_type=jnp.float32).astype(
        jnp.bfloat16
    )
    return (gate_up_grad, down_grad, input_grad)


def adam_update(weight, grad, first, second):
    first_new = beta_first * first + (1.0 - beta_first) * grad
    second_new = beta_second * second + (1.0 - beta_second) * grad * grad
    updated = (
        weight.astype(jnp.float32) - learn_rate * first_new / (jnp.sqrt(second_new) + adam_eps)
    ).astype(jnp.bfloat16)
    return (updated, first_new, second_new)


def exclusive_count(flags):
    n = flags.shape[-1]
    earlier = (jnp.arange(n)[:, None] < jnp.arange(n)[None, :]).astype(jnp.bfloat16)
    return jnp.dot(flags.astype(jnp.bfloat16), earlier, preferred_element_type=jnp.float32)


def local(
    tokens,
    cotangent,
    gate_probs,
    expert_ids,
    gate_up,
    down_weight,
    gate_up_moment,
    gate_up_second,
    down_moment,
    down_second,
):
    expert_count = lax.axis_size("expert")
    me = lax.axis_index("expert")
    local_tokens, model_width = tokens.shape
    top_count = expert_ids.shape[1]
    capacity = min(local_tokens, 9 * local_tokens * top_count // (4 * expert_count))
    slot_total = expert_count * capacity

    half_width = model_width // 2
    pieces = []
    rest = gate_probs
    for _ in range(3):
        piece = lax.reduce_precision(rest, exponent_bits=8, mantissa_bits=7)
        pieces.append(piece)
        rest = rest - piece
    meta = jnp.concatenate([expert_ids.astype(jnp.float32)] + pieces, axis=1)
    meta_width = 128
    meta = jnp.pad(meta, ((0, 0), (0, meta_width - meta.shape[1]))).astype(jnp.bfloat16)
    first = lax.all_gather(
        jnp.concatenate([tokens, cotangent[:, :half_width], meta], axis=1), "expert", axis=0
    )
    first, cot_after = lax.optimization_barrier((first, cotangent))
    cot_hi = lax.all_gather(cot_after[:, half_width:], "expert", axis=0)
    meta_at = model_width + half_width
    all_meta = first[..., meta_at : meta_at + 4 * top_count].astype(jnp.float32)
    all_ids = all_meta[..., :top_count].astype(jnp.int32)
    all_gates = (
        all_meta[..., top_count : 2 * top_count] + all_meta[..., 2 * top_count : 3 * top_count]
    ) + all_meta[..., 3 * top_count :]


    match = all_ids == me
    routed = jnp.any(match, axis=-1).astype(jnp.float32)
    gate_of = jnp.sum(jnp.where(match, all_gates, 0.0), axis=-1)
    rank = exclusive_count(routed)
    slots = jnp.arange(capacity, dtype=jnp.float32)
    pick = (routed[:, None, :] > 0) & (rank[:, None, :] == slots[None, :, None])
    pick_b = pick.astype(jnp.bfloat16)
    picked_first = jnp.einsum(
        "srt,stc->src", pick_b, first, preferred_element_type=jnp.float32
    ).astype(jnp.bfloat16)
    inputs = picked_first[..., :model_width]
    slot_gate = jnp.sum(jnp.where(pick, gate_of[:, None, :], 0.0), axis=-1)
    picked_hi = jnp.einsum(
        "srt,stc->src", pick_b, cot_hi, preferred_element_type=jnp.float32
    ).astype(jnp.bfloat16)
    scaled = [
        (slot_gate[..., None] * part.astype(jnp.float32))
        .astype(jnp.bfloat16)
        .reshape(slot_total, half_width)
        for part in (picked_first[..., model_width:meta_at], picked_hi)
    ]

    weight_pair = gate_up[0]
    weight_down = down_weight[0]
    grad_pair, grad_down, row_grads = expert_backward(
        inputs.reshape(slot_total, model_width),
        scaled,
        weight_pair,
        weight_down,
    )
    dense = jnp.einsum(
        "srt,src->stc",
        pick_b,
        row_grads.reshape(expert_count, capacity, model_width),
        preferred_element_type=jnp.float32,
    ).astype(jnp.bfloat16)
    token_grad = lax.psum_scatter(
        dense.reshape(expert_count * local_tokens, model_width),
        "expert",
        scatter_dimension=0,
        tiled=True,
    )

    groups = lax.axis_size("group")
    share_rows = model_width // groups
    hidden_count = grad_down.shape[0]
    pair_width = grad_pair.shape[1]
    pair_parts = lax.all_to_all(
        grad_pair.astype(jnp.bfloat16).reshape(groups, share_rows, pair_width),
        "group", 0, 0, tiled=True,
    )
    down_parts = lax.all_to_all(
        grad_down.astype(jnp.bfloat16).reshape(hidden_count, groups, share_rows),
        "group", 1, 1, tiled=True,
    )
    sum_pair = jnp.sum(pair_parts.astype(jnp.float32), axis=0)[None]
    sum_down = jnp.sum(down_parts.astype(jnp.float32), axis=1)[None]
    token_grad, sum_down = lax.optimization_barrier((token_grad, sum_down))
    group_index = lax.axis_index("group")
    own_pair = lax.dynamic_slice_in_dim(gate_up, group_index * share_rows, share_rows, 1)
    own_down = lax.dynamic_slice_in_dim(down_weight, group_index * share_rows, share_rows, 2)
    new_pair, first_pair, second_pair = adam_update(
        own_pair, sum_pair, gate_up_moment, gate_up_second
    )
    new_down, first_down, second_down = adam_update(own_down, sum_down, down_moment, down_second)
    full_pair = lax.all_to_all(
        jnp.broadcast_to(new_pair, (groups, share_rows, pair_width)), "group", 0, 0, tiled=True
    ).reshape(1, model_width, pair_width)
    full_down = lax.all_gather(new_down, "group", axis=2, tiled=True)
    return (token_grad, full_pair, full_down, first_pair, second_pair, first_down, second_down)


def solution(mesh):
    rows = P(("group", "expert"), None)
    placed = (
        rows,
        rows,
        rows,
        rows,
        P("expert", None, None),
        P("expert", None, None),
        P("expert", "group", None),
        P("expert", "group", None),
        P("expert", None, "group"),
        P("expert", None, "group"),
    )
    return jax.shard_map(
        local,
        mesh=mesh,
        in_specs=placed,
        out_specs=(
            rows,
            P("expert", None, None),
            P("expert", None, None),
            P("expert", "group", None),
            P("expert", "group", None),
            P("expert", None, "group"),
            P("expert", None, "group"),
        ),
        check_vma=False,
    )
```
